32 devices in a mesh: dp: 4 (over y, x), seq: 8 (over z, core).
Axes of the slice: x: 2, y: 2, z: 4, core: 2. Of those that a mesh axis runs over, the one named last changes fastest.
Arguments:
- asking_vectors_matrix: bfloat16 [4, 1024, 2048], P('dp', 'seq'), may hold values from -6 to 6
- matched_keys_matrix: bfloat16 [4, 1024, 2048], P('dp', 'seq'), may hold values from -6 to 6
- carried_vectors_matrix: bfloat16 [4, 1024, 2048], P('dp', 'seq'), may hold values from -6 to 6
- upstream_cotangent: bfloat16 [4, 1024, 2048], P('dp', 'seq'), may hold values from -6 to 6
- w_out: bfloat16 [2048, 2048], P('seq'), may hold values from -0.125 to 0.125
- panel_entry_offsets: int32 [4, 9], P('dp'), may hold values from 0 to 32, as said below
- rightward_panel_per_entry: int32 [4, 32], P('dp'), may hold values from 0 to 7, as said below
Outputs:
- layer_out: bfloat16 [4, 1024, 2048], P('dp', 'seq')
- q_grad: bfloat16 [4, 1024, 2048], P('dp', 'seq')
- k_grad: bfloat16 [4, 1024, 2048], P('dp', 'seq')
- v_grad: bfloat16 [4, 1024, 2048], P('dp', 'seq')
- w_out_grad: float32 [2048, 2048], P('seq')
The draws below stay inside these ranges and needn't reach their ends.
Inputs may be any that keep to these rules, and one draw needn't show every extreme that they name: panel_entry_offsets[b, 0] is 0 and panel_entry_offsets never falls along a row; tile row r owns slots panel_entry_offsets[b, r] to panel_entry_offsets[b, r + 1] - 1, 1 to 8 of them, and its own tile r is among its blocks; in every subgraph one tile row holds all 8 tiles; panel_entry_offsets[b, 8], the used slots, lies between 16 and 32 and equals 32 for at least one subgraph. `rightward_panel_per_entry`: the slots of a tile row hold distinct column tiles in rising order; slots from panel_entry_offsets[b, 8] on hold arbitrary tile numbers that take no part.
All inputs are finite; a program needn't handle non-finite values.
Results may differ from the reference program's by a relative error of at most 0.034.
Values may be sent and summed in bfloat16 or wider, within the bound.
No kernel may reach another device: no remote copies, remote signals or barrier semaphores. Data moves between devices by JAX's collectives and lax.ppermute only.
A program may use at most 128 MiB of HBM per device.

```python
import math
import jax
import jax.numpy as jnp
from jax import lax

H = 16
HD = 128
NODE_DEV = 128
EMBED_DIMENSION = 2048
NODES = 1024
TILES = 8
SLOTS = 32
BATCH = 4
N_SEQ = 8


def block_lists(key):
    tile_count = TILES
    slot_count = SLOTS
    batch_count = BATCH
    chosen_sub = jax.random.randint(jax.random.fold_in(key, 101), (), 0, batch_count)
    used = jax.random.randint(jax.random.fold_in(key, 102), (batch_count,), slot_count // 2, slot_count + 1)
    used = jnp.where(jnp.arange(batch_count, dtype=jnp.int32) == chosen_sub, slot_count, used)
    extra = used - tile_count
    row_weight = jnp.left_shift(jnp.int32(1), jax.random.randint(jax.random.fold_in(key, 103), (batch_count, tile_count), 0, 5))
    full_row = jax.random.randint(jax.random.fold_in(key, 104), (batch_count,), 0, tile_count)
    rows_at = jnp.arange(tile_count, dtype=jnp.int32)[:, None]
    cols_at = jnp.arange(tile_count, dtype=jnp.int32)[None, :]
    nearness = 1 + tile_count // (1 + jnp.abs(rows_at - cols_at))
    noise = jax.random.randint(jax.random.fold_in(key, 105), (batch_count, tile_count, tile_count), 1, 17)
    score = row_weight[:, :, None] * nearness[None] * noise
    lift = 256 * (tile_count + 1) + 1
    score = jnp.where(rows_at[None] == full_row[:, None, None], score + lift, score)
    perm_keys = jax.random.split(jax.random.fold_in(key, 106), batch_count)
    tiebreak = jax.vmap(lambda one_key: jax.random.permutation(one_key, tile_count * tile_count))(perm_keys)
    keyed = score * (tile_count * tile_count) + tiebreak.reshape(batch_count, tile_count, tile_count).astype(jnp.int32)
    on_diag = jnp.broadcast_to(rows_at == cols_at, (batch_count, tile_count, tile_count))
    keyed = jnp.where(on_diag, -1, keyed).reshape(batch_count, tile_count * tile_count)
    order = jnp.argsort(-keyed, axis=1)
    rank = jnp.argsort(order, axis=1)
    chosen = (rank < extra[:, None]) | on_diag.reshape(batch_count, tile_count * tile_count)
    counts = jnp.sum(chosen.reshape(batch_count, tile_count, tile_count).astype(jnp.int32), axis=2)
    starts = jnp.concatenate([jnp.zeros((batch_count, 1), jnp.int32), jnp.cumsum(counts, axis=1).astype(jnp.int32)], axis=1)
    position = jnp.cumsum(chosen.astype(jnp.int32), axis=1) - 1
    target = jnp.where(chosen, position, slot_count)
    filler = jax.random.randint(jax.random.fold_in(key, 107), (batch_count, slot_count + 1), 0, tile_count)
    column_of = jnp.broadcast_to(jnp.arange(tile_count * tile_count, dtype=jnp.int32) % tile_count, (batch_count, tile_count * tile_count))
    batch_rows = jnp.broadcast_to(jnp.arange(batch_count, dtype=jnp.int32)[:, None], (batch_count, tile_count * tile_count))
    columns = filler.at[batch_rows, target].set(column_of)[:, :slot_count]
    return (starts.astype(jnp.int32), columns.astype(jnp.int32))


def drawn_projections(key):
    shape = (BATCH, NODES, EMBED_DIMENSION)
    queries = jnp.clip(1.4 * jax.random.normal(jax.random.fold_in(key, 201), shape, jnp.float32), -6.0, 6.0)
    keyed_rows = jnp.clip(1.4 * jax.random.normal(jax.random.fold_in(key, 202), shape, jnp.float32), -6.0, 6.0)
    return (queries, keyed_rows)


def draw_asking_vectors_matrix(key, part):
    return drawn_projections(key)[0].astype(jnp.bfloat16)


def draw_matched_keys_matrix(key, part):
    return drawn_projections(key)[1].astype(jnp.bfloat16)


def draw_panel_entry_offsets(key, part):
    return block_lists(key)[0]


def draw_rightward_panel_per_entry(key, part):
    return block_lists(key)[1]


def levels(stream_key, shape, shards, least, top_value):
    loudness, own = 1.0, jax.random.fold_in(stream_key, 6)
    for axis_at, shards_of in shards:
        heights = jnp.exp(jax.random.uniform(jax.random.fold_in(own, axis_at), (shards_of,), jnp.float32, least / len(shards), top_value / len(shards)))
        loudness = loudness * jnp.repeat(heights, shape[axis_at] // shards_of).reshape([-1 if axis == axis_at else 1 for axis in range(len(shape))])
    return loudness


def gaussian(stream_key, extent, deviation, bound, shards=(), kind=jnp.bfloat16):
    entries = jax.random.normal(stream_key, extent, jnp.float32) * deviation
    if len(shards) > 0:
        entries = levels(stream_key, extent, shards, -0.22, 0.18) * entries
    return jnp.clip(entries, min=-bound, max=bound).astype(kind)


def setup_inputs(seed: int = 0) -> dict:
    streams_of = jax.random.split(jax.random.key(seed), 8)
    return {
        "asking_vectors_matrix": draw_asking_vectors_matrix(jax.random.fold_in(streams_of[7], 71), 0),
        "matched_keys_matrix": draw_matched_keys_matrix(jax.random.fold_in(streams_of[7], 71), 0),
        "carried_vectors_matrix": gaussian(streams_of[2], (BATCH, NODES, EMBED_DIMENSION), 1.0, 6.0, ((0, 4), (1, 8))),
        "upstream_cotangent": gaussian(streams_of[3], (BATCH, NODES, EMBED_DIMENSION), 1.0, 6.0, ((0, 4), (1, 8))),
        "w_out": gaussian(streams_of[4], (EMBED_DIMENSION, EMBED_DIMENSION), EMBED_DIMENSION ** -0.5, 0.125, ((0, 8),)),
        "panel_entry_offsets": draw_panel_entry_offsets(jax.random.fold_in(streams_of[7], 71), 0),
        "rightward_panel_per_entry": draw_rightward_panel_per_entry(jax.random.fold_in(streams_of[7], 71), 0),
    }


def entry_tables(starts, columns):
    tile_count = starts.shape[0] - 1
    slot_count = columns.shape[0]
    slot_index = jnp.arange(slot_count, dtype=jnp.int32)
    entry_row = lax.optimization_barrier(jnp.sum((starts[1:][None, :] <= slot_index[:, None]).astype(jnp.int32), axis=1)).astype(jnp.int32)
    in_use = entry_row < tile_count
    tile_ids = jnp.arange(tile_count, dtype=jnp.int32)
    row_hot = (entry_row[:, None] == tile_ids[None, :]).astype(jnp.float32)
    col_hot = jnp.where(in_use[:, None], (columns[:, None] == tile_ids[None, :]).astype(jnp.float32), 0.0)
    safe_row = jnp.minimum(entry_row, tile_count - 1).astype(jnp.int32)
    return (safe_row, in_use, row_hot, col_hot, columns)

def attend_forward(query_rows, key_rows, value_rows, tables):
    safe_row, in_use, row_hot, col_hot, columns = tables
    tile_count = row_hot.shape[1]
    tile_size = query_rows.shape[0] // tile_count
    head_depth = query_rows.shape[1]
    factor = 1.0 / math.sqrt(head_depth)
    top = lax.Precision.HIGHEST
    q_blocks = query_rows.reshape(tile_count, tile_size, head_depth)[safe_row].astype(jnp.float32)
    k_blocks = key_rows.reshape(tile_count, tile_size, head_depth)[columns].astype(jnp.float32)
    v_blocks = value_rows.reshape(tile_count, tile_size, head_depth)[columns].astype(jnp.float32)
    scores = jnp.einsum('eid,ejd->eij', q_blocks, k_blocks, precision=top) * factor
    block_max = lax.optimization_barrier(jnp.max(scores, axis=2))
    row_max = lax.optimization_barrier(jnp.max(jnp.where(row_hot[:, :, None] > 0, block_max[:, None, :], -jnp.inf), axis=0))
    expd = jnp.where(in_use[:, None, None], jnp.exp(scores - row_max[safe_row][:, :, None]), 0.0)
    row_total = jnp.einsum('er,ei->ri', row_hot, lax.optimization_barrier(jnp.sum(expd, axis=2)), precision=top)
    expd_low = expd.astype(jnp.bfloat16).astype(jnp.float32)
    weighted = jnp.einsum('eij,ejd->eid', expd_low, v_blocks, precision=top)
    summed = jnp.einsum('er,eid->rid', row_hot, weighted, precision=top)
    attended = (summed / row_total[:, :, None]).reshape(tile_count * tile_size, head_depth).astype(jnp.bfloat16)
    return (attended, row_max, row_total)

def attend_backward(query_rows, key_rows, value_rows, attended, grad_rows, row_max, row_total, tables):
    safe_row, in_use, row_hot, col_hot, columns = tables
    tile_count = row_hot.shape[1]
    tile_size = query_rows.shape[0] // tile_count
    head_depth = query_rows.shape[1]
    factor = 1.0 / math.sqrt(head_depth)
    top = lax.Precision.HIGHEST
    q_blocks = query_rows.reshape(tile_count, tile_size, head_depth)[safe_row].astype(jnp.float32)
    k_blocks = key_rows.reshape(tile_count, tile_size, head_depth)[columns].astype(jnp.float32)
    v_blocks = value_rows.reshape(tile_count, tile_size, head_depth)[columns].astype(jnp.float32)
    g_blocks = grad_rows.reshape(tile_count, tile_size, head_depth)[safe_row].astype(jnp.float32)
    scores = jnp.einsum('eid,ejd->eij', q_blocks, k_blocks, precision=top) * factor
    prob = jnp.where(in_use[:, None, None], jnp.exp(scores - row_max[safe_row][:, :, None]) / row_total[safe_row][:, :, None], 0.0)
    prob_low = prob.astype(jnp.bfloat16).astype(jnp.float32)
    v_terms = jnp.einsum('eij,eid->ejd', prob_low, g_blocks, precision=top)
    v_sum = jnp.einsum('er,ejd->rjd', col_hot, v_terms, precision=top)
    prob_grad = jnp.einsum('eid,ejd->eij', g_blocks, v_blocks, precision=top)
    delta = lax.optimization_barrier(jnp.sum(attended.astype(jnp.float32) * grad_rows.astype(jnp.float32), axis=1)).reshape(tile_count, tile_size)
    score_grad = (prob * (prob_grad - delta[safe_row][:, :, None]) * factor).astype(jnp.bfloat16).astype(jnp.float32)
    q_terms = jnp.einsum('eij,ejd->eid', score_grad, k_blocks, precision=top)
    q_sum = jnp.einsum('er,eid->rid', row_hot, q_terms, precision=top)
    k_terms = jnp.einsum('eij,eid->ejd', score_grad, q_blocks, precision=top)
    k_sum = jnp.einsum('er,ejd->rjd', col_hot, k_terms, precision=top)
    node_count = tile_count * tile_size
    return (q_sum.reshape(node_count, head_depth).astype(jnp.bfloat16), k_sum.reshape(node_count, head_depth).astype(jnp.bfloat16), v_sum.reshape(node_count, head_depth).astype(jnp.bfloat16))

def reference(asking_vectors_matrix, matched_keys_matrix, carried_vectors_matrix, upstream_cotangent, w_out, panel_entry_offsets, rightward_panel_per_entry):

    def head_major(values):
        return values.reshape(NODES, H, HD).transpose(1, 0, 2)

    def node_major(values):
        return values.transpose(1, 0, 2).reshape(NODES, EMBED_DIMENSION)

    def lone_cluster_piece(coefficient_aggregate, incoming_features):
        queries, keys_here, values_here, grads_here, starts, columns = incoming_features
        tables = entry_tables(starts, columns)

        def forward_head(items):
            return attend_forward(items[0], items[1], items[2], tables)
        head_q = head_major(queries)
        head_k = head_major(keys_here)
        head_v = head_major(values_here)
        attended_heads, row_max, row_total = lax.map(forward_head, (head_q, head_k, head_v))
        attended = node_major(attended_heads)
        layer = jnp.dot(attended, w_out, preferred_element_type=jnp.float32).astype(jnp.bfloat16)
        attended_grad = lax.dot_general(grads_here, w_out, (((1,), (1,)), ((), ())), preferred_element_type=jnp.float32).astype(jnp.bfloat16)
        grad_heads = head_major(attended_grad)

        def backward_head(items):
            return attend_backward(items[0], items[1], items[2], items[3], items[4], items[5], items[6], tables)
        q_heads, k_heads, v_heads = lax.map(backward_head, (head_q, head_k, head_v, attended_heads, grad_heads, row_max, row_total))

        def add_into_patch(running, pair):
            term = lax.dot_general(pair[0], pair[1], (((0,), (0,)), ((), ())), preferred_element_type=jnp.float32).astype(jnp.bfloat16)
            term = lax.optimization_barrier(term)
            return (running + term.astype(jnp.float32), None)
        softmax_patches = attended.reshape(N_SEQ, NODE_DEV, EMBED_DIMENSION)
        derivative_patches = grads_here.reshape(N_SEQ, NODE_DEV, EMBED_DIMENSION)
        cluster_piece_count, discarded_thing = lax.scan(add_into_patch, jnp.zeros((EMBED_DIMENSION, EMBED_DIMENSION), jnp.float32), (softmax_patches, derivative_patches))
        produced_features = (layer, node_major(q_heads), node_major(k_heads), node_major(v_heads))
        return (coefficient_aggregate + cluster_piece_count, produced_features)
    coefficient_aggregate, produced_features = lax.scan(lone_cluster_piece, jnp.zeros((EMBED_DIMENSION, EMBED_DIMENSION), jnp.float32), (asking_vectors_matrix, matched_keys_matrix, carried_vectors_matrix, upstream_cotangent, panel_entry_offsets, rightward_panel_per_entry))
    return (produced_features[0], produced_features[1], produced_features[2], produced_features[3], coefficient_aggregate / BATCH)
```

```python
import math

import jax
import jax.numpy as jnp
from jax import lax
from jax.sharding import PartitionSpec as P

H = 16
HD = 128


def tile_mask(starts, columns, nodes):
    tile_count = starts.shape[0] - 1
    slot_count = columns.shape[0]
    tile_size = nodes // tile_count
    slot_index = jnp.arange(slot_count, dtype=jnp.int32)
    entry_row = jnp.sum((starts[1:][None, :] <= slot_index[:, None]).astype(jnp.int32), axis=1)
    tile_ids = jnp.arange(tile_count, dtype=jnp.int32)
    row_hot = (entry_row[:, None] == tile_ids[None, :]).astype(jnp.int32)
    col_hot = (columns[:, None] == tile_ids[None, :]).astype(jnp.int32)
    pairs = jnp.einsum("er,ec->rc", row_hot, col_hot) > 0
    full = jnp.broadcast_to(
        pairs[:, None, :, None], (tile_count, tile_size, tile_count, tile_size)
    )
    return full.reshape(nodes, nodes)


def attend(q, k, v, g, allowed):
    factor = 1.0 / math.sqrt(q.shape[-1])
    scores = jnp.einsum("ihd,jhd->hij", q, k, preferred_element_type=jnp.float32) * factor
    masked = jnp.where(allowed[None], scores, -jnp.inf)
    row_max = jnp.max(masked, axis=2, keepdims=True)
    expd = jnp.where(allowed[None], jnp.exp(scores - row_max), 0.0)
    row_total = jnp.sum(expd, axis=2, keepdims=True)
    weighted = jnp.einsum(
        "hij,jhd->ihd", expd.astype(jnp.bfloat16), v, preferred_element_type=jnp.float32
    )
    totals = jnp.transpose(row_total[:, :, 0])[:, :, None]
    attended = (weighted / totals).astype(jnp.bfloat16)
    return attended, expd, row_total


def attend_back(q, k, v, g, attended, expd, row_total):
    factor = 1.0 / math.sqrt(q.shape[-1])
    prob = expd / row_total
    prob_low = prob.astype(jnp.bfloat16)
    v_grad = jnp.einsum("hij,ihd->jhd", prob_low, g, preferred_element_type=jnp.float32)
    prob_grad = jnp.einsum("ihd,jhd->hij", g, v, preferred_element_type=jnp.float32)
    delta = jnp.sum(attended.astype(jnp.float32) * g.astype(jnp.float32), axis=2)
    delta = jnp.transpose(delta)[:, :, None]
    score_grad = (prob * (prob_grad - delta) * factor).astype(jnp.bfloat16)
    q_grad = jnp.einsum("hij,jhd->ihd", score_grad, k, preferred_element_type=jnp.float32)
    k_grad = jnp.einsum("hij,ihd->jhd", score_grad, q, preferred_element_type=jnp.float32)
    return (
        q_grad.astype(jnp.bfloat16),
        k_grad.astype(jnp.bfloat16),
        v_grad.astype(jnp.bfloat16),
    )


def shards(
    asking_vectors_matrix,
    matched_keys_matrix,
    carried_vectors_matrix,
    upstream_cotangent,
    w_out,
    panel_entry_offsets,
    rightward_panel_per_entry,
):
    nodes_here = asking_vectors_matrix.shape[1]
    width = asking_vectors_matrix.shape[2]
    n_seq = lax.axis_size("seq")
    nodes = nodes_here * n_seq

    grad_here = upstream_cotangent[0]
    grad_full = lax.all_gather(grad_here, "seq", axis=0, tiled=True)
    w_full = lax.all_gather(w_out, "seq", axis=0, tiled=True)

    stacked = jnp.stack(
        [asking_vectors_matrix[0], matched_keys_matrix[0], carried_vectors_matrix[0]]
    ).reshape(3, nodes_here, H, HD)
    heads = lax.all_to_all(stacked, "seq", split_axis=2, concat_axis=1, tiled=True)
    q_heads, k_heads, v_heads = heads[0], heads[1], heads[2]
    local_heads = q_heads.shape[1]

    allowed = tile_mask(panel_entry_offsets[0], rightward_panel_per_entry[0], nodes)

    g_flat = lax.dot_general(
        grad_full, w_out, (((1,), (1,)), ((), ())), preferred_element_type=jnp.float32
    ).astype(jnp.bfloat16)
    g_heads = g_flat.reshape(nodes, local_heads, HD)

    attended, expd, row_total = attend(q_heads, k_heads, v_heads, g_heads, allowed)

    returned = lax.all_to_all(attended, "seq", split_axis=0, concat_axis=1, tiled=True)
    attended_nodes = returned.reshape(nodes_here, width)
    layer_out = jnp.dot(attended_nodes, w_full, preferred_element_type=jnp.float32)
    layer_out = layer_out.astype(jnp.bfloat16)[None]

    att_blocks = attended.reshape(n_seq, nodes_here, local_heads * HD)
    grad_blocks = grad_full.reshape(n_seq, nodes_here, width)
    terms = jnp.einsum(
        "bnf,bnk->bfk", att_blocks, grad_blocks, preferred_element_type=jnp.float32
    ).astype(jnp.bfloat16)
    w_rows = jnp.sum(terms.astype(jnp.float32), axis=0)
    batch = asking_vectors_matrix.shape[0] * lax.axis_size("dp")
    w_out_grad = lax.psum(w_rows, "dp") / batch

    q_g, k_g, v_g = attend_back(q_heads, k_heads, v_heads, g_heads, attended, expd, row_total)
    grads = jnp.stack([q_g, k_g, v_g])
    back = lax.all_to_all(grads, "seq", split_axis=1, concat_axis=2, tiled=True)
    back = back.reshape(3, 1, nodes_here, width)
    return (layer_out, back[0], back[1], back[2], w_out_grad)


def solution(mesh):
    return jax.shard_map(
        shards,
        mesh=mesh,
        in_specs=(
            P("dp", "seq", None),
            P("dp", "seq", None),
            P("dp", "seq", None),
            P("dp", "seq", None),
            P("seq", None),
            P("dp", None),
            P("dp", None),
        ),
        out_specs=(
            P("dp", "seq", None),
            P("dp", "seq", None),
            P("dp", "seq", None),
            P("dp", "seq", None),
            P("seq", None),
        ),
        check_vma=False,
    )
```

```python
import math

import jax
import jax.numpy as jnp
from jax import lax
from jax.sharding import PartitionSpec as P

H = 16
HD = 128


def tile_mask(starts, columns, nodes):
    tile_count = starts.shape[0] - 1
    slot_count = columns.shape[0]
    tile_size = nodes // tile_count
    slot_index = jnp.arange(slot_count, dtype=jnp.int32)
    entry_row = jnp.sum((starts[1:][None, :] <= slot_index[:, None]).astype(jnp.int32), axis=1)
    tile_ids = jnp.arange(tile_count, dtype=jnp.int32)
    row_hot = (entry_row[:, None] == tile_ids[None, :]).astype(jnp.int32)
    col_hot = (columns[:, None] == tile_ids[None, :]).astype(jnp.int32)
    pairs = jnp.einsum("er,ec->rc", row_hot, col_hot) > 0
    full = jnp.broadcast_to(
        pairs[:, None, :, None], (tile_count, tile_size, tile_count, tile_size)
    )
    return full.reshape(nodes, nodes)


def attend(q, k, v, g, allowed):
    factor = 1.0 / math.sqrt(q.shape[-1])
    scores = jnp.einsum("ihd,jhd->hij", q, k, preferred_element_type=jnp.float32) * factor
    masked = jnp.where(allowed[None], scores, -jnp.inf)
    row_max = jnp.max(masked, axis=2, keepdims=True)
    expd = jnp.where(allowed[None], jnp.exp(scores - row_max), 0.0)
    row_total = jnp.sum(expd, axis=2, keepdims=True)
    weighted = jnp.einsum(
        "hij,jhd->ihd", expd.astype(jnp.bfloat16), v, preferred_element_type=jnp.float32
    )
    totals = jnp.transpose(row_total[:, :, 0])[:, :, None]
    attended = (weighted / totals).astype(jnp.bfloat16)
    return attended, expd, row_total


def attend_back(q, k, v, g, attended, expd, row_total):
    factor = 1.0 / math.sqrt(q.shape[-1])
    prob = expd / row_total
    prob_low = prob.astype(jnp.bfloat16)
    v_grad = jnp.einsum("hij,ihd->jhd", prob_low, g, preferred_element_type=jnp.float32)
    prob_grad = jnp.einsum("ihd,jhd->hij", g, v, preferred_element_type=jnp.float32)
    delta = jnp.sum(attended.astype(jnp.float32) * g.astype(jnp.float32), axis=2)
    delta = jnp.transpose(delta)[:, :, None]
    score_grad = (prob * (prob_grad - delta) * factor).astype(jnp.bfloat16)
    q_grad = jnp.einsum("hij,jhd->ihd", score_grad, k, preferred_element_type=jnp.float32)
    k_grad = jnp.einsum("hij,ihd->jhd", score_grad, q, preferred_element_type=jnp.float32)
    return (
        q_grad.astype(jnp.bfloat16),
        k_grad.astype(jnp.bfloat16),
        v_grad.astype(jnp.bfloat16),
    )


def dp_sum(values):
    n_dp = lax.axis_size("dp")
    if n_dp & (n_dp - 1):
        return lax.psum(values, "dp")
    step = 1
    while step < n_dp:
        pairs = [(i, i ^ step) for i in range(n_dp)]
        values = values + lax.ppermute(values, "dp", pairs)
        step *= 2
    return values


def shards(
    asking_vectors_matrix,
    matched_keys_matrix,
    carried_vectors_matrix,
    upstream_cotangent,
    w_out,
    panel_entry_offsets,
    rightward_panel_per_entry,
):
    nodes_here = asking_vectors_matrix.shape[1]
    width = asking_vectors_matrix.shape[2]
    n_seq = lax.axis_size("seq")
    nodes = nodes_here * n_seq

    grad_here = upstream_cotangent[0]
    grad_full = lax.all_gather(grad_here, "seq", axis=0, tiled=True)

    stacked = jnp.stack(
        [asking_vectors_matrix[0], matched_keys_matrix[0], carried_vectors_matrix[0]]
    ).reshape(3, nodes_here, H, HD)
    heads = lax.all_to_all(stacked, "seq", split_axis=2, concat_axis=1, tiled=True)
    q_heads, k_heads, v_heads = heads[0], heads[1], heads[2]
    local_heads = q_heads.shape[1]

    allowed = tile_mask(panel_entry_offsets[0], rightward_panel_per_entry[0], nodes)

    attended, expd, row_total = attend(q_heads, k_heads, v_heads, None, allowed)
    att_flat = attended.reshape(nodes, local_heads * HD)

    partial = jnp.dot(att_flat, w_out, preferred_element_type=jnp.float32)
    layer_out = lax.psum_scatter(
        partial.astype(jnp.bfloat16), "seq", scatter_dimension=0, tiled=True
    )[None]

    g_flat = lax.dot_general(
        grad_full, w_out, (((1,), (1,)), ((), ())), preferred_element_type=jnp.float32
    ).astype(jnp.bfloat16)
    g_heads = g_flat.reshape(nodes, local_heads, HD)

    att_blocks = att_flat.reshape(n_seq, nodes_here, local_heads * HD)
    grad_blocks = grad_full.reshape(n_seq, nodes_here, width)
    terms = jnp.einsum(
        "bnf,bnk->bfk", att_blocks, grad_blocks, preferred_element_type=jnp.float32
    ).astype(jnp.bfloat16)
    w_rows = jnp.sum(terms.astype(jnp.float32), axis=0)
    w_rows = dp_sum(w_rows)
    batch = asking_vectors_matrix.shape[0] * lax.axis_size("dp")
    w_out_grad = w_rows / batch

    q_g, k_g, v_g = attend_back(q_heads, k_heads, v_heads, g_heads, attended, expd, row_total)
    grads = jnp.stack([q_g, k_g, v_g])
    back = lax.all_to_all(grads, "seq", split_axis=1, concat_axis=2, tiled=True)
    back = back.reshape(3, 1, nodes_here, width)
    return (layer_out, back[0], back[1], back[2], w_out_grad)


def solution(mesh):
    return jax.shard_map(
        shards,
        mesh=mesh,
        in_specs=(
            P("dp", "seq", None),
            P("dp", "seq", None),
            P("dp", "seq", None),
            P("dp", "seq", None),
            P("seq", None),
            P("dp", None),
            P("dp", None),
        ),
        out_specs=(
            P("dp", "seq", None),
            P("dp", "seq", None),
            P("dp", "seq", None),
            P("dp", "seq", None),
            P("seq", None),
        ),
        check_vma=False,
    )
```

```python
import math

import jax
import jax.numpy as jnp
from jax import lax
from jax.sharding import PartitionSpec as P

H = 16
HD = 128


def tile_mask(starts, columns, nodes):
    tile_count = starts.shape[0] - 1
    slot_count = columns.shape[0]
    tile_size = nodes // tile_count
    slot_index = jnp.arange(slot_count, dtype=jnp.int32)
    entry_row = jnp.sum((starts[1:][None, :] <= slot_index[:, None]).astype(jnp.int32), axis=1)
    tile_ids = jnp.arange(tile_count, dtype=jnp.int32)
    row_hot = (entry_row[:, None] == tile_ids[None, :]).astype(jnp.int32)
    col_hot = (columns[:, None] == tile_ids[None, :]).astype(jnp.int32)
    pairs = jnp.einsum("er,ec->rc", row_hot, col_hot) > 0
    full = jnp.broadcast_to(
        pairs[:, None, :, None], (tile_count, tile_size, tile_count, tile_size)
    )
    return full.reshape(nodes, nodes)


def attend(q, k, v, g, allowed):
    factor = 1.0 / math.sqrt(q.shape[-1])
    scores = jnp.einsum("ihd,jhd->hij", q, k, preferred_element_type=jnp.float32) * factor
    masked = jnp.where(allowed[None], scores, -jnp.inf)
    row_max = jnp.max(masked, axis=2, keepdims=True)
    expd = jnp.where(allowed[None], jnp.exp(scores - row_max), 0.0)
    row_total = jnp.sum(expd, axis=2, keepdims=True)
    weighted = jnp.einsum(
        "hij,jhd->ihd", expd.astype(jnp.bfloat16), v, preferred_element_type=jnp.float32
    )
    totals = jnp.transpose(row_total[:, :, 0])[:, :, None]
    attended = (weighted / totals).astype(jnp.bfloat16)
    return attended, expd, row_total


def attend_back(q, k, v, g, attended, expd, row_total):
    factor = 1.0 / math.sqrt(q.shape[-1])
    prob = expd / row_total
    prob_low = prob.astype(jnp.bfloat16)
    v_grad = jnp.einsum("hij,ihd->jhd", prob_low, g, preferred_element_type=jnp.float32)
    prob_grad = jnp.einsum("ihd,jhd->hij", g, v, preferred_element_type=jnp.float32)
    delta = jnp.sum(attended.astype(jnp.float32) * g.astype(jnp.float32), axis=2)
    delta = jnp.transpose(delta)[:, :, None]
    score_grad = (prob * (prob_grad - delta) * factor).astype(jnp.bfloat16)
    q_grad = jnp.einsum("hij,jhd->ihd", score_grad, k, preferred_element_type=jnp.float32)
    k_grad = jnp.einsum("hij,ihd->jhd", score_grad, q, preferred_element_type=jnp.float32)
    return (
        q_grad.astype(jnp.bfloat16),
        k_grad.astype(jnp.bfloat16),
        v_grad.astype(jnp.bfloat16),
    )


def dp_sum(values):
    n_dp = lax.axis_size("dp")
    if n_dp & (n_dp - 1):
        return lax.psum(values, "dp")
    step = 1
    while step < n_dp:
        pairs = [(i, i ^ step) for i in range(n_dp)]
        values = values + lax.ppermute(values, "dp", pairs)
        step *= 2
    return values


def seq_reduce_scatter(partial):
    n = lax.axis_size("seq")
    rows = partial.shape[0] // n
    if n % 2:
        return lax.psum_scatter(partial, "seq", scatter_dimension=0, tiled=True)
    chips = n // 2
    s = lax.axis_index("seq")
    core = s % 2
    z = s // 2
    halves = partial.reshape(chips, 2, rows, partial.shape[1])
    mine = jnp.where(core == 0, halves[:, 0], halves[:, 1])
    other = jnp.where(core == 0, halves[:, 1], halves[:, 0])
    got = lax.ppermute(other.astype(jnp.bfloat16), "seq", [(i, i ^ 1) for i in range(n)])
    chip = mine + got.astype(jnp.float32)
    own = lax.dynamic_index_in_dim(chip, z, 0, keepdims=False)
    right = [(i, i + 2) for i in range(n - 2)]
    left = [(i, i - 2) for i in range(2, n)]
    recv_r = None
    recv_l = None
    for step in range(1, chips):
        d_r = jnp.clip(z + chips - step, 0, chips - 1)
        d_l = jnp.clip(z - chips + step, 0, chips - 1)
        acc_r = lax.dynamic_index_in_dim(chip, d_r, 0, keepdims=False)
        acc_l = lax.dynamic_index_in_dim(chip, d_l, 0, keepdims=False)
        if recv_r is not None:
            ok_r = (step >= z + 1) & (z >= 1)
            ok_l = (step >= chips - z) & (z <= chips - 2)
            acc_r = acc_r + jnp.where(ok_r, recv_r.astype(jnp.float32), 0.0)
            acc_l = acc_l + jnp.where(ok_l, recv_l.astype(jnp.float32), 0.0)
        recv_r = lax.ppermute(acc_r.astype(jnp.bfloat16), "seq", right)
        recv_l = lax.ppermute(acc_l.astype(jnp.bfloat16), "seq", left)
    total = own
    if recv_r is not None:
        total = total + jnp.where(z >= 1, recv_r.astype(jnp.float32), 0.0)
        total = total + jnp.where(z <= chips - 2, recv_l.astype(jnp.float32), 0.0)
    return total


def shards(
    asking_vectors_matrix,
    matched_keys_matrix,
    carried_vectors_matrix,
    upstream_cotangent,
    w_out,
    panel_entry_offsets,
    rightward_panel_per_entry,
):
    nodes_here = asking_vectors_matrix.shape[1]
    width = asking_vectors_matrix.shape[2]
    n_seq = lax.axis_size("seq")
    nodes = nodes_here * n_seq

    grad_here = upstream_cotangent[0]
    grad_full = lax.all_gather(grad_here, "seq", axis=0, tiled=True)

    stacked = jnp.stack(
        [asking_vectors_matrix[0], matched_keys_matrix[0], carried_vectors_matrix[0]]
    ).reshape(3, nodes_here, H, HD)
    heads = lax.all_to_all(stacked, "seq", split_axis=2, concat_axis=1, tiled=True)
    q_heads, k_heads, v_heads = heads[0], heads[1], heads[2]
    local_heads = q_heads.shape[1]

    allowed = tile_mask(panel_entry_offsets[0], rightward_panel_per_entry[0], nodes)

    attended, expd, row_total = attend(q_heads, k_heads, v_heads, None, allowed)
    att_flat = attended.reshape(nodes, local_heads * HD)

    partial = jnp.dot(att_flat, w_out, preferred_element_type=jnp.float32)
    layer_out = seq_reduce_scatter(partial).astype(jnp.bfloat16)[None]

    g_flat = lax.dot_general(
        grad_full, w_out, (((1,), (1,)), ((), ())), preferred_element_type=jnp.float32
    ).astype(jnp.bfloat16)
    g_heads = g_flat.reshape(nodes, local_heads, HD)

    att_blocks = att_flat.reshape(n_seq, nodes_here, local_heads * HD)
    grad_blocks = grad_full.reshape(n_seq, nodes_here, width)
    terms = jnp.einsum(
        "bnf,bnk->bfk", att_blocks, grad_blocks, preferred_element_type=jnp.float32
    ).astype(jnp.bfloat16)
    w_rows = jnp.sum(terms.astype(jnp.float32), axis=0)
    w_rows = dp_sum(w_rows)
    batch = asking_vectors_matrix.shape[0] * lax.axis_size("dp")
    w_out_grad = w_rows / batch

    q_g, k_g, v_g = attend_back(q_heads, k_heads, v_heads, g_heads, attended, expd, row_total)
    grads = jnp.stack([q_g, k_g, v_g])
    back = lax.all_to_all(grads, "seq", split_axis=1, concat_axis=2, tiled=True)
    back = back.reshape(3, 1, nodes_here, width)
    return (layer_out, back[0], back[1], back[2], w_out_grad)


def solution(mesh):
    return jax.shard_map(
        shards,
        mesh=mesh,
        in_specs=(
            P("dp", "seq", None),
            P("dp", "seq", None),
            P("dp", "seq", None),
            P("dp", "seq", None),
            P("seq", None),
            P("dp", None),
            P("dp", None),
        ),
        out_specs=(
            P("dp", "seq", None),
            P("dp", "seq", None),
            P("dp", "seq", None),
            P("dp", "seq", None),
            P("seq", None),
        ),
        check_vma=False,
    )
```

```python
import math

import jax
import jax.numpy as jnp
from jax import lax
from jax.sharding import PartitionSpec as P

H = 16
HD = 128


def tile_mask(starts, columns, nodes):
    tile_count = starts.shape[0] - 1
    slot_count = columns.shape[0]
    tile_size = nodes // tile_count
    slot_index = jnp.arange(slot_count, dtype=jnp.int32)
    entry_row = jnp.sum((starts[1:][None, :] <= slot_index[:, None]).astype(jnp.int32), axis=1)
    tile_ids = jnp.arange(tile_count, dtype=jnp.int32)
    row_hot = (entry_row[:, None] == tile_ids[None, :]).astype(jnp.int32)
    col_hot = (columns[:, None] == tile_ids[None, :]).astype(jnp.int32)
    pairs = jnp.einsum("er,ec->rc", row_hot, col_hot) > 0
    full = jnp.broadcast_to(
        pairs[:, None, :, None], (tile_count, tile_size, tile_count, tile_size)
    )
    return full.reshape(nodes, nodes)


def attend(q, k, v, allowed):
    factor = 1.0 / math.sqrt(q.shape[-1])
    scores = jnp.dot(q, k.T, preferred_element_type=jnp.float32) * factor
    masked = jnp.where(allowed, scores, -jnp.inf)
    row_max = jnp.max(masked, axis=1, keepdims=True)
    expd = jnp.where(allowed, jnp.exp(scores - row_max), 0.0)
    row_total = jnp.sum(expd, axis=1, keepdims=True)
    weighted = jnp.dot(expd.astype(jnp.bfloat16), v, preferred_element_type=jnp.float32)
    attended = (weighted / row_total).astype(jnp.bfloat16)
    return attended, expd, row_total


def attend_back(q, k, v, g, attended, expd, row_total):
    factor = 1.0 / math.sqrt(q.shape[-1])
    prob = expd / row_total
    prob_low = prob.astype(jnp.bfloat16)
    v_grad = jnp.dot(prob_low.T, g, preferred_element_type=jnp.float32)
    prob_grad = jnp.dot(g, v.T, preferred_element_type=jnp.float32)
    delta = jnp.sum(
        attended.astype(jnp.float32) * g.astype(jnp.float32), axis=1, keepdims=True
    )
    score_grad = (prob * (prob_grad - delta) * factor).astype(jnp.bfloat16)
    q_grad = jnp.dot(score_grad, k, preferred_element_type=jnp.float32)
    k_grad = jnp.dot(score_grad.T, q, preferred_element_type=jnp.float32)
    return (
        q_grad.astype(jnp.bfloat16),
        k_grad.astype(jnp.bfloat16),
        v_grad.astype(jnp.bfloat16),
    )


def dp_sum(values):
    n_dp = lax.axis_size("dp")
    if n_dp & (n_dp - 1):
        return lax.psum(values, "dp")
    step = 1
    while step < n_dp:
        pairs = [(i, i ^ step) for i in range(n_dp)]
        values = values + lax.ppermute(values, "dp", pairs)
        step *= 2
    return values


def shards(
    asking_vectors_matrix,
    matched_keys_matrix,
    carried_vectors_matrix,
    upstream_cotangent,
    w_out,
    panel_entry_offsets,
    rightward_panel_per_entry,
):
    nodes_here = asking_vectors_matrix.shape[1]
    width = asking_vectors_matrix.shape[2]
    n_seq = lax.axis_size("seq")
    nodes = nodes_here * n_seq

    grad_here = upstream_cotangent[0]
    grad_full = lax.all_gather(grad_here, "seq", axis=0, tiled=True)

    groups = n_seq
    group_width = width // groups
    local_heads = group_width // HD

    def to_groups(values):
        return values.reshape(nodes_here, groups, group_width).transpose(1, 0, 2)

    stacked = jnp.stack(
        [
            to_groups(asking_vectors_matrix[0]),
            to_groups(matched_keys_matrix[0]),
            to_groups(carried_vectors_matrix[0]),
        ]
    )
    heads = lax.all_to_all(stacked, "seq", split_axis=1, concat_axis=1, tiled=True)
    heads = heads.reshape(3, nodes, group_width)

    allowed = tile_mask(panel_entry_offsets[0], rightward_panel_per_entry[0], nodes)

    def head_cols(values, h):
        return values[:, h * HD : (h + 1) * HD]

    fwd = [
        attend(head_cols(heads[0], h), head_cols(heads[1], h), head_cols(heads[2], h), allowed)
        for h in range(local_heads)
    ]
    att_flat = jnp.concatenate([f[0] for f in fwd], axis=1)

    partial = jnp.dot(att_flat, w_out, preferred_element_type=jnp.float32)
    layer_out = lax.psum_scatter(
        partial.astype(jnp.bfloat16), "seq", scatter_dimension=0, tiled=True
    )[None]

    g_flat = lax.dot_general(
        grad_full, w_out, (((1,), (1,)), ((), ())), preferred_element_type=jnp.float32
    ).astype(jnp.bfloat16)
    att_blocks = att_flat.reshape(n_seq, nodes_here, local_heads * HD)
    grad_blocks = grad_full.reshape(n_seq, nodes_here, width)
    terms = jnp.einsum(
        "bnf,bnk->bfk", att_blocks, grad_blocks, preferred_element_type=jnp.float32
    ).astype(jnp.bfloat16)
    w_rows = jnp.sum(terms.astype(jnp.float32), axis=0)
    w_rows = dp_sum(w_rows)
    batch = asking_vectors_matrix.shape[0] * lax.axis_size("dp")
    w_out_grad = w_rows / batch

    bwd = [
        attend_back(
            head_cols(heads[0], h),
            head_cols(heads[1], h),
            head_cols(heads[2], h),
            head_cols(g_flat, h),
            fwd[h][0],
            fwd[h][1],
            fwd[h][2],
        )
        for h in range(local_heads)
    ]
    grads = jnp.stack(
        [jnp.concatenate([b[i] for b in bwd], axis=1).reshape(groups, nodes_here, group_width)
         for i in range(3)]
    )
    back = lax.all_to_all(grads, "seq", split_axis=1, concat_axis=1, tiled=True)
    back = back.transpose(0, 2, 1, 3).reshape(3, 1, nodes_here, width)
    return (layer_out, back[0], back[1], back[2], w_out_grad)


def solution(mesh):
    return jax.shard_map(
        shards,
        mesh=mesh,
        in_specs=(
            P("dp", "seq", None),
            P("dp", "seq", None),
            P("dp", "seq", None),
            P("dp", "seq", None),
            P("seq", None),
            P("dp", None),
            P("dp", None),
        ),
        out_specs=(
            P("dp", "seq", None),
            P("dp", "seq", None),
            P("dp", "seq", None),
            P("dp", "seq", None),
            P("seq", None),
        ),
        check_vma=False,
    )
```

```python
import math

import jax
import jax.numpy as jnp
from jax import lax
from jax.sharding import PartitionSpec as P

H = 16
HD = 128


def tile_mask(starts, columns, nodes):
    tile_count = starts.shape[0] - 1
    slot_count = columns.shape[0]
    tile_size = nodes // tile_count
    slot_index = jnp.arange(slot_count, dtype=jnp.int32)
    entry_row = jnp.sum((starts[1:][None, :] <= slot_index[:, None]).astype(jnp.int32), axis=1)
    tile_ids = jnp.arange(tile_count, dtype=jnp.int32)
    row_hot = (entry_row[:, None] == tile_ids[None, :]).astype(jnp.int32)
    col_hot = (columns[:, None] == tile_ids[None, :]).astype(jnp.int32)
    pairs = jnp.einsum("er,ec->rc", row_hot, col_hot) > 0
    full = jnp.broadcast_to(
        pairs[:, None, :, None], (tile_count, tile_size, tile_count, tile_size)
    )
    return full.reshape(nodes, nodes)


def attend(q, k, v, allowed):
    factor = 1.0 / math.sqrt(q.shape[-1])
    scores = jnp.dot(q, k.T, preferred_element_type=jnp.float32) * factor
    masked = jnp.where(allowed, scores, -jnp.inf)
    row_max = jnp.max(masked, axis=1, keepdims=True)
    expd = jnp.where(allowed, jnp.exp(scores - row_max), 0.0)
    row_total = jnp.sum(expd, axis=1, keepdims=True)
    weighted = jnp.dot(expd.astype(jnp.bfloat16), v, preferred_element_type=jnp.float32)
    attended = (weighted / row_total).astype(jnp.bfloat16)
    return attended, expd, row_total


def attend_back(q, k, v, g, attended, expd, row_total):
    factor = 1.0 / math.sqrt(q.shape[-1])
    prob = expd / row_total
    prob_low = prob.astype(jnp.bfloat16)
    v_grad = jnp.dot(prob_low.T, g, preferred_element_type=jnp.float32)
    prob_grad = jnp.dot(g, v.T, preferred_element_type=jnp.float32)
    delta = jnp.sum(
        attended.astype(jnp.float32) * g.astype(jnp.float32), axis=1, keepdims=True
    )
    score_grad = (prob * (prob_grad - delta) * factor).astype(jnp.bfloat16)
    q_grad = jnp.dot(score_grad, k, preferred_element_type=jnp.float32)
    k_grad = jnp.dot(score_grad.T, q, preferred_element_type=jnp.float32)
    return (
        q_grad.astype(jnp.bfloat16),
        k_grad.astype(jnp.bfloat16),
        v_grad.astype(jnp.bfloat16),
    )


def dp_sum(values):
    n_dp = lax.axis_size("dp")
    if n_dp & (n_dp - 1):
        return lax.psum(values, "dp")
    step = 1
    while step < n_dp:
        pairs = [(i, i ^ step) for i in range(n_dp)]
        values = values + lax.ppermute(values, "dp", pairs)
        step *= 2
    return values


def line_gather(x):
    n = lax.axis_size("seq")
    chips = n // 2
    s = lax.axis_index("seq")
    core = s % 2
    z = s // 2
    right = [(i, i + 2) for i in range(n - 2)]
    left = [(i, i - 2) for i in range(2, n)]
    before = []
    after = []
    r = x
    l = x
    for step in range(1, chips):
        r = lax.ppermute(r, "seq", right)
        l = lax.ppermute(l, "seq", left)
        before.append(r)
        after.append(l)
    rel = jnp.stack(before[::-1] + [x] + after)
    mine = lax.dynamic_slice_in_dim(rel, chips - 1 - z, chips, axis=0)
    other = lax.ppermute(mine, "seq", [(i, i ^ 1) for i in range(n)])
    return mine, other, core


def pair_rows(first, second, core):
    pair = jnp.where(
        core == 0, jnp.stack([first, second], axis=1), jnp.stack([second, first], axis=1)
    )
    return pair


def shards(
    asking_vectors_matrix,
    matched_keys_matrix,
    carried_vectors_matrix,
    upstream_cotangent,
    w_out,
    panel_entry_offsets,
    rightward_panel_per_entry,
):
    nodes_here = asking_vectors_matrix.shape[1]
    width = asking_vectors_matrix.shape[2]
    n_seq = lax.axis_size("seq")
    nodes = nodes_here * n_seq

    grad_here = upstream_cotangent[0]
    up_mine, up_other, core = line_gather(grad_here)

    groups = n_seq
    group_width = width // groups
    local_heads = group_width // HD

    def to_groups(values):
        return values.reshape(nodes_here, groups, group_width).transpose(1, 0, 2)

    stacked = jnp.stack(
        [
            to_groups(asking_vectors_matrix[0]),
            to_groups(matched_keys_matrix[0]),
            to_groups(carried_vectors_matrix[0]),
        ]
    )
    heads = lax.all_to_all(stacked, "seq", split_axis=1, concat_axis=1, tiled=True)
    heads = heads.reshape(3, nodes, group_width)

    allowed = tile_mask(panel_entry_offsets[0], rightward_panel_per_entry[0], nodes)

    def head_cols(values, h):
        return values[:, h * HD : (h + 1) * HD]

    fwd = [
        attend(head_cols(heads[0], h), head_cols(heads[1], h), head_cols(heads[2], h), allowed)
        for h in range(local_heads)
    ]
    att_flat = jnp.concatenate([f[0] for f in fwd], axis=1)

    partial = jnp.dot(att_flat, w_out, preferred_element_type=jnp.float32)
    layer_out = lax.psum_scatter(
        partial.astype(jnp.bfloat16), "seq", scatter_dimension=0, tiled=True
    )[None]

    def times_w(values):
        return lax.dot_general(
            values, w_out, (((2,), (1,)), ((), ())), preferred_element_type=jnp.float32
        ).astype(jnp.bfloat16)

    g_flat = pair_rows(times_w(up_mine), times_w(up_other), core).reshape(nodes, group_width)

    att4 = att_flat.reshape(n_seq // 2, 2, nodes_here, group_width)
    att_mine = jnp.where(core == 0, att4[:, 0], att4[:, 1])
    att_other = jnp.where(core == 0, att4[:, 1], att4[:, 0])

    def block_terms(att_part, up_part):
        return jnp.einsum(
            "bnf,bnk->bfk", att_part, up_part, preferred_element_type=jnp.float32
        ).astype(jnp.bfloat16)

    w_rows = jnp.sum(block_terms(att_mine, up_mine).astype(jnp.float32), axis=0) + jnp.sum(
        block_terms(att_other, up_other).astype(jnp.float32), axis=0
    )
    w_rows = dp_sum(w_rows)
    batch = asking_vectors_matrix.shape[0] * lax.axis_size("dp")
    w_out_grad = w_rows / batch

    bwd = [
        attend_back(
            head_cols(heads[0], h),
            head_cols(heads[1], h),
            head_cols(heads[2], h),
            head_cols(g_flat, h),
            fwd[h][0],
            fwd[h][1],
            fwd[h][2],
        )
        for h in range(local_heads)
    ]
    grads = jnp.stack(
        [jnp.concatenate([b[i] for b in bwd], axis=1).reshape(groups, nodes_here, group_width)
         for i in range(3)]
    )
    back = lax.all_to_all(grads, "seq", split_axis=1, concat_axis=1, tiled=True)
    back = back.transpose(0, 2, 1, 3).reshape(3, 1, nodes_here, width)
    return (layer_out, back[0], back[1], back[2], w_out_grad)


def solution(mesh):
    return jax.shard_map(
        shards,
        mesh=mesh,
        in_specs=(
            P("dp", "seq", None),
            P("dp", "seq", None),
            P("dp", "seq", None),
            P("dp", "seq", None),
            P("seq", None),
            P("dp", None),
            P("dp", None),
        ),
        out_specs=(
            P("dp", "seq", None),
            P("dp", "seq", None),
            P("dp", "seq", None),
            P("dp", "seq", None),
            P("seq", None),
        ),
        check_vma=False,
    )
```

```python
import math

import jax
import jax.numpy as jnp
from jax import lax
from jax.sharding import PartitionSpec as P

H = 16
HD = 128


def tile_mask(starts, columns, nodes):
    tile_count = starts.shape[0] - 1
    slot_count = columns.shape[0]
    tile_size = nodes // tile_count
    slot_index = jnp.arange(slot_count, dtype=jnp.int32)
    entry_row = jnp.sum((starts[1:][None, :] <= slot_index[:, None]).astype(jnp.int32), axis=1)
    tile_ids = jnp.arange(tile_count, dtype=jnp.int32)
    row_hot = (entry_row[:, None] == tile_ids[None, :]).astype(jnp.int32)
    col_hot = (columns[:, None] == tile_ids[None, :]).astype(jnp.int32)
    pairs = jnp.einsum("er,ec->rc", row_hot, col_hot) > 0
    full = jnp.broadcast_to(
        pairs[:, None, :, None], (tile_count, tile_size, tile_count, tile_size)
    )
    return full.reshape(nodes, nodes)


def attend(q, k, v, allowed):
    factor = 1.0 / math.sqrt(q.shape[-1])
    scores = jnp.dot(q, k.T, preferred_element_type=jnp.float32) * factor
    masked = jnp.where(allowed, scores, -jnp.inf)
    row_max = jnp.max(masked, axis=1, keepdims=True)
    expd = jnp.where(allowed, jnp.exp(scores - row_max), 0.0)
    row_total = jnp.sum(expd, axis=1, keepdims=True)
    weighted = jnp.dot(expd.astype(jnp.bfloat16), v, preferred_element_type=jnp.float32)
    attended = (weighted / row_total).astype(jnp.bfloat16)
    return attended, expd, row_total


def attend_back(q, k, v, g, attended, expd, row_total):
    factor = 1.0 / math.sqrt(q.shape[-1])
    prob = expd / row_total
    prob_low = prob.astype(jnp.bfloat16)
    v_grad = jnp.dot(prob_low.T, g, preferred_element_type=jnp.float32)
    prob_grad = jnp.dot(g, v.T, preferred_element_type=jnp.float32)
    delta = jnp.sum(
        attended.astype(jnp.float32) * g.astype(jnp.float32), axis=1, keepdims=True
    )
    score_grad = (prob * (prob_grad - delta) * factor).astype(jnp.bfloat16)
    q_grad = jnp.dot(score_grad, k, preferred_element_type=jnp.float32)
    k_grad = jnp.dot(score_grad.T, q, preferred_element_type=jnp.float32)
    return (
        q_grad.astype(jnp.bfloat16),
        k_grad.astype(jnp.bfloat16),
        v_grad.astype(jnp.bfloat16),
    )


def dp_sum(values):
    n_dp = lax.axis_size("dp")
    if n_dp & (n_dp - 1):
        return lax.psum(values, "dp")
    step = 1
    while step < n_dp:
        pairs = [(i, i ^ step) for i in range(n_dp)]
        values = values + lax.ppermute(values, "dp", pairs)
        step *= 2
    return values


def chip_layer_out(att_flat, w_out):
    n = lax.axis_size("seq")
    rows = att_flat.shape[0] // n
    chips = n // 2
    s = lax.axis_index("seq")
    core = s % 2
    z = s // 2
    sibling = [(i, i ^ 1) for i in range(n)]
    att_sib = lax.ppermute(att_flat, "seq", sibling)
    w_sib = lax.ppermute(w_out, "seq", sibling)

    def parity_rows(values):
        quads = values.reshape(chips, 2, rows, values.shape[1])
        return jnp.where(core == 0, quads[:, 0], quads[:, 1])

    att_chip = jnp.concatenate([parity_rows(att_flat), parity_rows(att_sib)], axis=2)
    w_chip = jnp.concatenate([w_out, w_sib], axis=0)
    chip_partial = lax.dot_general(
        att_chip, w_chip, (((2,), (0,)), ((), ())), preferred_element_type=jnp.float32
    )
    total = lax.dynamic_index_in_dim(chip_partial, z, 0, keepdims=False)
    sent = chip_partial.astype(jnp.bfloat16)
    for k in range(1, chips):
        pairs = [(i, ((i // 2 + k) % chips) * 2 + i % 2) for i in range(n)]
        piece = lax.dynamic_index_in_dim(sent, (z + k) % chips, 0, keepdims=False)
        total = total + lax.ppermute(piece, "seq", pairs).astype(jnp.float32)
    return total


def shards(
    asking_vectors_matrix,
    matched_keys_matrix,
    carried_vectors_matrix,
    upstream_cotangent,
    w_out,
    panel_entry_offsets,
    rightward_panel_per_entry,
):
    nodes_here = asking_vectors_matrix.shape[1]
    width = asking_vectors_matrix.shape[2]
    n_seq = lax.axis_size("seq")
    nodes = nodes_here * n_seq

    grad_here = upstream_cotangent[0]
    grad_full = lax.all_gather(grad_here, "seq", axis=0, tiled=True)

    groups = n_seq
    group_width = width // groups
    local_heads = group_width // HD

    def to_groups(values):
        return values.reshape(nodes_here, groups, group_width).transpose(1, 0, 2)

    stacked = jnp.stack(
        [
            to_groups(asking_vectors_matrix[0]),
            to_groups(matched_keys_matrix[0]),
            to_groups(carried_vectors_matrix[0]),
        ]
    )
    heads = lax.all_to_all(stacked, "seq", split_axis=1, concat_axis=1, tiled=True)
    heads = heads.reshape(3, nodes, group_width)

    allowed = tile_mask(panel_entry_offsets[0], rightward_panel_per_entry[0], nodes)

    def head_cols(values, h):
        return values[:, h * HD : (h + 1) * HD]

    fwd = [
        attend(head_cols(heads[0], h), head_cols(heads[1], h), head_cols(heads[2], h), allowed)
        for h in range(local_heads)
    ]
    att_flat = jnp.concatenate([f[0] for f in fwd], axis=1)

    layer_out = chip_layer_out(att_flat, w_out).astype(jnp.bfloat16)[None]

    g_flat = lax.dot_general(
        grad_full, w_out, (((1,), (1,)), ((), ())), preferred_element_type=jnp.float32
    ).astype(jnp.bfloat16)
    att_blocks = att_flat.reshape(n_seq, nodes_here, local_heads * HD)
    grad_blocks = grad_full.reshape(n_seq, nodes_here, width)
    terms = jnp.einsum(
        "bnf,bnk->bfk", att_blocks, grad_blocks, preferred_element_type=jnp.float32
    ).astype(jnp.bfloat16)
    w_rows = jnp.sum(terms.astype(jnp.float32), axis=0)
    w_rows = dp_sum(w_rows)
    batch = asking_vectors_matrix.shape[0] * lax.axis_size("dp")
    w_out_grad = w_rows / batch

    bwd = [
        attend_back(
            head_cols(heads[0], h),
            head_cols(heads[1], h),
            head_cols(heads[2], h),
            head_cols(g_flat, h),
            fwd[h][0],
            fwd[h][1],
            fwd[h][2],
        )
        for h in range(local_heads)
    ]
    grads = jnp.stack(
        [jnp.concatenate([b[i] for b in bwd], axis=1).reshape(groups, nodes_here, group_width)
         for i in range(3)]
    )
    back = lax.all_to_all(grads, "seq", split_axis=1, concat_axis=1, tiled=True)
    back = back.transpose(0, 2, 1, 3).reshape(3, 1, nodes_here, width)
    return (layer_out, back[0], back[1], back[2], w_out_grad)


def solution(mesh):
    return jax.shard_map(
        shards,
        mesh=mesh,
        in_specs=(
            P("dp", "seq", None),
            P("dp", "seq", None),
            P("dp", "seq", None),
            P("dp", "seq", None),
            P("seq", None),
            P("dp", None),
            P("dp", None),
        ),
        out_specs=(
            P("dp", "seq", None),
            P("dp", "seq", None),
            P("dp", "seq", None),
            P("dp", "seq", None),
            P("seq", None),
        ),
        check_vma=False,
    )
```

```python
import math

import jax
import jax.numpy as jnp
from jax import lax
from jax.sharding import PartitionSpec as P

H = 16
HD = 128


def tile_mask(starts, columns, nodes):
    tile_count = starts.shape[0] - 1
    slot_count = columns.shape[0]
    tile_size = nodes // tile_count
    slot_index = jnp.arange(slot_count, dtype=jnp.int32)
    entry_row = jnp.sum((starts[1:][None, :] <= slot_index[:, None]).astype(jnp.int32), axis=1)
    tile_ids = jnp.arange(tile_count, dtype=jnp.int32)
    row_hot = (entry_row[:, None] == tile_ids[None, :]).astype(jnp.int32)
    col_hot = (columns[:, None] == tile_ids[None, :]).astype(jnp.int32)
    pairs = jnp.einsum("er,ec->rc", row_hot, col_hot) > 0
    full = jnp.broadcast_to(
        pairs[:, None, :, None], (tile_count, tile_size, tile_count, tile_size)
    )
    return full.reshape(nodes, nodes)


def attend(q, k, v, allowed):
    factor = 1.0 / math.sqrt(q.shape[-1])
    scores = jnp.dot(q, k.T, preferred_element_type=jnp.float32) * factor
    masked = jnp.where(allowed, scores, -jnp.inf)
    row_max = jnp.max(masked, axis=1, keepdims=True)
    expd = jnp.where(allowed, jnp.exp(scores - row_max), 0.0)
    row_total = jnp.sum(expd, axis=1, keepdims=True)
    weighted = jnp.dot(expd.astype(jnp.bfloat16), v, preferred_element_type=jnp.float32)
    attended = (weighted / row_total).astype(jnp.bfloat16)
    return attended, expd, row_total


def attend_back(q, k, v, g, attended, expd, row_total):
    factor = 1.0 / math.sqrt(q.shape[-1])
    prob = expd / row_total
    prob_low = prob.astype(jnp.bfloat16)
    v_grad = jnp.dot(prob_low.T, g, preferred_element_type=jnp.float32)
    prob_grad = jnp.dot(g, v.T, preferred_element_type=jnp.float32)
    delta = jnp.sum(
        attended.astype(jnp.float32) * g.astype(jnp.float32), axis=1, keepdims=True
    )
    score_grad = (prob * (prob_grad - delta) * factor).astype(jnp.bfloat16)
    q_grad = jnp.dot(score_grad, k, preferred_element_type=jnp.float32)
    k_grad = jnp.dot(score_grad.T, q, preferred_element_type=jnp.float32)
    return (
        q_grad.astype(jnp.bfloat16),
        k_grad.astype(jnp.bfloat16),
        v_grad.astype(jnp.bfloat16),
    )


def chip_layer_out(att_flat, w_out):
    n = lax.axis_size("seq")
    rows = att_flat.shape[0] // n
    chips = n // 2
    s = lax.axis_index("seq")
    core = s % 2
    z = s // 2
    sibling = [(i, i ^ 1) for i in range(n)]
    att_sib = lax.ppermute(att_flat, "seq", sibling)
    w_sib = lax.ppermute(w_out, "seq", sibling)

    def parity_rows(values):
        quads = values.reshape(chips, 2, rows, values.shape[1])
        return jnp.where(core == 0, quads[:, 0], quads[:, 1])

    att_chip = jnp.concatenate([parity_rows(att_flat), parity_rows(att_sib)], axis=2)
    w_chip = jnp.concatenate([w_out, w_sib], axis=0)
    chip_partial = lax.dot_general(
        att_chip, w_chip, (((2,), (0,)), ((), ())), preferred_element_type=jnp.float32
    )
    total = lax.dynamic_index_in_dim(chip_partial, z, 0, keepdims=False)
    sent = chip_partial.astype(jnp.bfloat16)
    for k in range(1, chips):
        pairs = [(i, ((i // 2 + k) % chips) * 2 + i % 2) for i in range(n)]
        piece = lax.dynamic_index_in_dim(sent, (z + k) % chips, 0, keepdims=False)
        total = total + lax.ppermute(piece, "seq", pairs).astype(jnp.float32)
    return total


def shards(
    asking_vectors_matrix,
    matched_keys_matrix,
    carried_vectors_matrix,
    upstream_cotangent,
    w_out,
    panel_entry_offsets,
    rightward_panel_per_entry,
):
    nodes_here = asking_vectors_matrix.shape[1]
    width = asking_vectors_matrix.shape[2]
    n_seq = lax.axis_size("seq")
    nodes = nodes_here * n_seq

    grad_here = upstream_cotangent[0]
    grad_full = lax.all_gather(grad_here, "seq", axis=0, tiled=True)

    groups = n_seq
    group_width = width // groups
    local_heads = group_width // HD

    def to_groups(values):
        return values.reshape(nodes_here, groups, group_width).transpose(1, 0, 2)

    stacked = jnp.stack(
        [
            to_groups(asking_vectors_matrix[0]),
            to_groups(matched_keys_matrix[0]),
            to_groups(carried_vectors_matrix[0]),
        ]
    )
    heads = lax.all_to_all(stacked, "seq", split_axis=1, concat_axis=1, tiled=True)
    heads = heads.reshape(3, nodes, group_width)

    allowed = tile_mask(panel_entry_offsets[0], rightward_panel_per_entry[0], nodes)

    def head_cols(values, h):
        return values[:, h * HD : (h + 1) * HD]

    fwd = [
        attend(head_cols(heads[0], h), head_cols(heads[1], h), head_cols(heads[2], h), allowed)
        for h in range(local_heads)
    ]
    att_flat = jnp.concatenate([f[0] for f in fwd], axis=1)

    layer_out = chip_layer_out(att_flat, w_out).astype(jnp.bfloat16)[None]

    g_flat = lax.dot_general(
        grad_full, w_out, (((1,), (1,)), ((), ())), preferred_element_type=jnp.float32
    ).astype(jnp.bfloat16)
    att_blocks = att_flat.reshape(n_seq, nodes_here, local_heads * HD)
    grad_blocks = grad_full.reshape(n_seq, nodes_here, width)
    terms = jnp.einsum(
        "bnf,bnk->bfk", att_blocks, grad_blocks, preferred_element_type=jnp.float32
    ).astype(jnp.bfloat16)
    w_rows = jnp.sum(terms.astype(jnp.float32), axis=0)
    w_rows = lax.psum(w_rows.astype(jnp.bfloat16), "dp").astype(jnp.float32)
    batch = asking_vectors_matrix.shape[0] * lax.axis_size("dp")
    w_out_grad = w_rows / batch

    bwd = [
        attend_back(
            head_cols(heads[0], h),
            head_cols(heads[1], h),
            head_cols(heads[2], h),
            head_cols(g_flat, h),
            fwd[h][0],
            fwd[h][1],
            fwd[h][2],
        )
        for h in range(local_heads)
    ]
    grads = jnp.stack(
        [jnp.concatenate([b[i] for b in bwd], axis=1).reshape(groups, nodes_here, group_width)
         for i in range(3)]
    )
    back = lax.all_to_all(grads, "seq", split_axis=1, concat_axis=1, tiled=True)
    back = back.transpose(0, 2, 1, 3).reshape(3, 1, nodes_here, width)
    return (layer_out, back[0], back[1], back[2], w_out_grad)


def solution(mesh):
    return jax.shard_map(
        shards,
        mesh=mesh,
        in_specs=(
            P("dp", "seq", None),
            P("dp", "seq", None),
            P("dp", "seq", None),
            P("dp", "seq", None),
            P("seq", None),
            P("dp", None),
            P("dp", None),
        ),
        out_specs=(
            P("dp", "seq", None),
            P("dp", "seq", None),
            P("dp", "seq", None),
            P("dp", "seq", None),
            P("seq", None),
        ),
        check_vma=False,
    )
```

```python
import math

import jax
import jax.numpy as jnp
from jax import lax
from jax.sharding import PartitionSpec as P

H = 16
HD = 128


def tile_mask(starts, columns, nodes):
    tile_count = starts.shape[0] - 1
    slot_count = columns.shape[0]
    tile_size = nodes // tile_count
    slot_index = jnp.arange(slot_count, dtype=jnp.int32)
    entry_row = jnp.sum((starts[1:][None, :] <= slot_index[:, None]).astype(jnp.int32), axis=1)
    tile_ids = jnp.arange(tile_count, dtype=jnp.int32)
    row_hot = (entry_row[:, None] == tile_ids[None, :]).astype(jnp.int32)
    col_hot = (columns[:, None] == tile_ids[None, :]).astype(jnp.int32)
    pairs = jnp.einsum("er,ec->rc", row_hot, col_hot) > 0
    full = jnp.broadcast_to(
        pairs[:, None, :, None], (tile_count, tile_size, tile_count, tile_size)
    )
    return full.reshape(nodes, nodes)


def attend(q, k, v, allowed):
    factor = 1.0 / math.sqrt(q.shape[-1])
    scores = jnp.dot(q, k.T, preferred_element_type=jnp.float32) * factor
    masked = jnp.where(allowed, scores, -jnp.inf)
    row_max = jnp.max(masked, axis=1, keepdims=True)
    expd = jnp.where(allowed, jnp.exp(scores - row_max), 0.0)
    row_total = jnp.sum(expd, axis=1, keepdims=True)
    weighted = jnp.dot(expd.astype(jnp.bfloat16), v, preferred_element_type=jnp.float32)
    attended = (weighted / row_total).astype(jnp.bfloat16)
    return attended, expd, row_total


def attend_back(q, k, v, g, attended, expd, row_total):
    factor = 1.0 / math.sqrt(q.shape[-1])
    prob = expd / row_total
    prob_low = prob.astype(jnp.bfloat16)
    v_grad = jnp.dot(prob_low.T, g, preferred_element_type=jnp.float32)
    prob_grad = jnp.dot(g, v.T, preferred_element_type=jnp.float32)
    delta = jnp.sum(
        attended.astype(jnp.float32) * g.astype(jnp.float32), axis=1, keepdims=True
    )
    score_grad = (prob * (prob_grad - delta) * factor).astype(jnp.bfloat16)
    q_grad = jnp.dot(score_grad, k, preferred_element_type=jnp.float32)
    k_grad = jnp.dot(score_grad.T, q, preferred_element_type=jnp.float32)
    return (
        q_grad.astype(jnp.bfloat16),
        k_grad.astype(jnp.bfloat16),
        v_grad.astype(jnp.bfloat16),
    )


def chip_gather(x):
    n = lax.axis_size("seq")
    chips = n // 2
    s = lax.axis_index("seq")
    core = s % 2
    z = s // 2
    pieces = [x]
    for k in range(1, chips):
        pairs = [(i, ((i // 2 + k) % chips) * 2 + i % 2) for i in range(n)]
        pieces.append(lax.ppermute(x, "seq", pairs))
    by_shift = jnp.stack(pieces)
    order = (z - jnp.arange(chips, dtype=jnp.int32)) % chips
    mine = jnp.take(by_shift, order, axis=0)
    other = lax.ppermute(mine, "seq", [(i, i ^ 1) for i in range(n)])
    return mine, other, core


def pair_rows(first, second, core):
    return jnp.where(
        core == 0, jnp.stack([first, second], axis=1), jnp.stack([second, first], axis=1)
    )


def chip_layer_out(att_flat, w_out):
    n = lax.axis_size("seq")
    rows = att_flat.shape[0] // n
    chips = n // 2
    s = lax.axis_index("seq")
    core = s % 2
    z = s // 2
    sibling = [(i, i ^ 1) for i in range(n)]
    att_sib = lax.ppermute(att_flat, "seq", sibling)
    w_sib = lax.ppermute(w_out, "seq", sibling)

    def parity_rows(values):
        quads = values.reshape(chips, 2, rows, values.shape[1])
        return jnp.where(core == 0, quads[:, 0], quads[:, 1])

    att_chip = jnp.concatenate([parity_rows(att_flat), parity_rows(att_sib)], axis=2)
    w_chip = jnp.concatenate([w_out, w_sib], axis=0)
    chip_partial = lax.dot_general(
        att_chip, w_chip, (((2,), (0,)), ((), ())), preferred_element_type=jnp.float32
    )
    total = lax.dynamic_index_in_dim(chip_partial, z, 0, keepdims=False)
    sent = chip_partial.astype(jnp.bfloat16)
    for k in range(1, chips):
        pairs = [(i, ((i // 2 + k) % chips) * 2 + i % 2) for i in range(n)]
        piece = lax.dynamic_index_in_dim(sent, (z + k) % chips, 0, keepdims=False)
        total = total + lax.ppermute(piece, "seq", pairs).astype(jnp.float32)
    return total


def shards(
    asking_vectors_matrix,
    matched_keys_matrix,
    carried_vectors_matrix,
    upstream_cotangent,
    w_out,
    panel_entry_offsets,
    rightward_panel_per_entry,
):
    nodes_here = asking_vectors_matrix.shape[1]
    width = asking_vectors_matrix.shape[2]
    n_seq = lax.axis_size("seq")
    nodes = nodes_here * n_seq

    grad_here = upstream_cotangent[0]
    up_mine, up_other, core = chip_gather(grad_here)

    groups = n_seq
    group_width = width // groups
    local_heads = group_width // HD

    def to_groups(values):
        return values.reshape(nodes_here, groups, group_width).transpose(1, 0, 2)

    stacked = jnp.stack(
        [
            to_groups(asking_vectors_matrix[0]),
            to_groups(matched_keys_matrix[0]),
            to_groups(carried_vectors_matrix[0]),
        ]
    )
    heads = lax.all_to_all(stacked, "seq", split_axis=1, concat_axis=1, tiled=True)
    heads = heads.reshape(3, nodes, group_width)

    allowed = tile_mask(panel_entry_offsets[0], rightward_panel_per_entry[0], nodes)

    def head_cols(values, h):
        return values[:, h * HD : (h + 1) * HD]

    fwd = [
        attend(head_cols(heads[0], h), head_cols(heads[1], h), head_cols(heads[2], h), allowed)
        for h in range(local_heads)
    ]
    att_flat = jnp.concatenate([f[0] for f in fwd], axis=1)

    layer_out = chip_layer_out(att_flat, w_out).astype(jnp.bfloat16)[None]

    def times_w(values):
        return lax.dot_general(
            values, w_out, (((2,), (1,)), ((), ())), preferred_element_type=jnp.float32
        ).astype(jnp.bfloat16)

    g_flat = pair_rows(times_w(up_mine), times_w(up_other), core).reshape(nodes, group_width)

    att4 = att_flat.reshape(n_seq // 2, 2, nodes_here, group_width)
    att_mine = jnp.where(core == 0, att4[:, 0], att4[:, 1])
    att_other = jnp.where(core == 0, att4[:, 1], att4[:, 0])

    def block_terms(att_part, up_part):
        return jnp.einsum(
            "bnf,bnk->bfk", att_part, up_part, preferred_element_type=jnp.float32
        ).astype(jnp.bfloat16)

    w_rows = jnp.sum(block_terms(att_mine, up_mine).astype(jnp.float32), axis=0) + jnp.sum(
        block_terms(att_other, up_other).astype(jnp.float32), axis=0
    )
    w_rows = lax.psum(w_rows.astype(jnp.bfloat16), "dp").astype(jnp.float32)
    batch = asking_vectors_matrix.shape[0] * lax.axis_size("dp")
    w_out_grad = w_rows / batch

    bwd = [
        attend_back(
            head_cols(heads[0], h),
            head_cols(heads[1], h),
            head_cols(heads[2], h),
            head_cols(g_flat, h),
            fwd[h][0],
            fwd[h][1],
            fwd[h][2],
        )
        for h in range(local_heads)
    ]
    grads = jnp.stack(
        [jnp.concatenate([b[i] for b in bwd], axis=1).reshape(groups, nodes_here, group_width)
         for i in range(3)]
    )
    back = lax.all_to_all(grads, "seq", split_axis=1, concat_axis=1, tiled=True)
    back = back.transpose(0, 2, 1, 3).reshape(3, 1, nodes_here, width)
    return (layer_out, back[0], back[1], back[2], w_out_grad)


def solution(mesh):
    return jax.shard_map(
        shards,
        mesh=mesh,
        in_specs=(
            P("dp", "seq", None),
            P("dp", "seq", None),
            P("dp", "seq", None),
            P("dp", "seq", None),
            P("seq", None),
            P("dp", None),
            P("dp", None),
        ),
        out_specs=(
            P("dp", "seq", None),
            P("dp", "seq", None),
            P("dp", "seq", None),
            P("dp", "seq", None),
            P("seq", None),
        ),
        check_vma=False,
    )
```

```python
import math

import jax
import jax.numpy as jnp
from jax import lax
from jax.sharding import PartitionSpec as P

H = 16
HD = 128


def tile_mask(starts, columns, nodes):
    tile_count = starts.shape[0] - 1
    slot_count = columns.shape[0]
    tile_size = nodes // tile_count
    slot_index = jnp.arange(slot_count, dtype=jnp.int32)
    entry_row = jnp.sum((starts[1:][None, :] <= slot_index[:, None]).astype(jnp.int32), axis=1)
    tile_ids = jnp.arange(tile_count, dtype=jnp.int32)
    row_hot = (entry_row[:, None] == tile_ids[None, :]).astype(jnp.int32)
    col_hot = (columns[:, None] == tile_ids[None, :]).astype(jnp.int32)
    pairs = jnp.einsum("er,ec->rc", row_hot, col_hot) > 0
    full = jnp.broadcast_to(
        pairs[:, None, :, None], (tile_count, tile_size, tile_count, tile_size)
    )
    return full.reshape(nodes, nodes)


def attend(q, k, v, allowed):
    factor = 1.0 / math.sqrt(q.shape[-1])
    scores = jnp.dot(q, k.T, preferred_element_type=jnp.float32) * factor
    masked = jnp.where(allowed, scores, -jnp.inf)
    row_max = jnp.max(masked, axis=1, keepdims=True)
    expd = jnp.where(allowed, jnp.exp(scores - row_max), 0.0)
    row_total = jnp.sum(expd, axis=1, keepdims=True)
    weighted = jnp.dot(expd.astype(jnp.bfloat16), v, preferred_element_type=jnp.float32)
    attended = (weighted / row_total).astype(jnp.bfloat16)
    return attended, expd, row_total


def attend_back(q, k, v, g, attended, expd, row_total):
    factor = 1.0 / math.sqrt(q.shape[-1])
    prob = expd / row_total
    prob_low = prob.astype(jnp.bfloat16)
    v_grad = jnp.dot(prob_low.T, g, preferred_element_type=jnp.float32)
    prob_grad = jnp.dot(g, v.T, preferred_element_type=jnp.float32)
    delta = jnp.sum(
        attended.astype(jnp.float32) * g.astype(jnp.float32), axis=1, keepdims=True
    )
    score_grad = (prob * (prob_grad - delta) * factor).astype(jnp.bfloat16)
    q_grad = jnp.dot(score_grad, k, preferred_element_type=jnp.float32)
    k_grad = jnp.dot(score_grad.T, q, preferred_element_type=jnp.float32)
    return (
        q_grad.astype(jnp.bfloat16),
        k_grad.astype(jnp.bfloat16),
        v_grad.astype(jnp.bfloat16),
    )


def chip_gather(x):
    n = lax.axis_size("seq")
    chips = n // 2
    s = lax.axis_index("seq")
    core = s % 2
    z = s // 2
    right = [(i, i + 2) for i in range(n - 2)]
    left = [(i, i - 2) for i in range(2, n)]
    before = []
    after = []
    r = x
    l = x
    for step in range(1, chips):
        r = lax.ppermute(r, "seq", right)
        l = lax.ppermute(l, "seq", left)
        before.append(r)
        after.append(l)
    rel = jnp.stack(before[::-1] + [x] + after)
    mine = lax.dynamic_slice_in_dim(rel, chips - 1 - z, chips, axis=0)
    other = lax.ppermute(mine, "seq", [(i, i ^ 1) for i in range(n)])
    return mine, other, core


def pair_rows(first, second, core):
    return jnp.where(
        core == 0, jnp.stack([first, second], axis=1), jnp.stack([second, first], axis=1)
    )


def chip_layer_out(att_flat, w_out):
    n = lax.axis_size("seq")
    rows = att_flat.shape[0] // n
    chips = n // 2
    s = lax.axis_index("seq")
    core = s % 2
    z = s // 2
    sibling = [(i, i ^ 1) for i in range(n)]
    att_sib = lax.ppermute(att_flat, "seq", sibling)
    w_sib = lax.ppermute(w_out, "seq", sibling)

    def parity_rows(values):
        quads = values.reshape(chips, 2, rows, values.shape[1])
        return jnp.where(core == 0, quads[:, 0], quads[:, 1])

    att_chip = jnp.concatenate([parity_rows(att_flat), parity_rows(att_sib)], axis=2)
    w_chip = jnp.concatenate([w_out, w_sib], axis=0)
    chip_partial = lax.dot_general(
        att_chip, w_chip, (((2,), (0,)), ((), ())), preferred_element_type=jnp.float32
    )
    own = lax.dynamic_index_in_dim(chip_partial, z, 0, keepdims=False)
    right = [(i, i + 2) for i in range(n - 2)]
    left = [(i, i - 2) for i in range(2, n)]
    recv_r = None
    recv_l = None
    for step in range(1, chips):
        d_r = jnp.clip(z + chips - step, 0, chips - 1)
        d_l = jnp.clip(z - chips + step, 0, chips - 1)
        acc_r = lax.dynamic_index_in_dim(chip_partial, d_r, 0, keepdims=False)
        acc_l = lax.dynamic_index_in_dim(chip_partial, d_l, 0, keepdims=False)
        if recv_r is not None:
            ok_r = (step >= z + 1) & (z >= 1)
            ok_l = (step >= chips - z) & (z <= chips - 2)
            acc_r = acc_r + jnp.where(ok_r, recv_r.astype(jnp.float32), 0.0)
            acc_l = acc_l + jnp.where(ok_l, recv_l.astype(jnp.float32), 0.0)
        recv_r = lax.ppermute(acc_r.astype(jnp.bfloat16), "seq", right)
        recv_l = lax.ppermute(acc_l.astype(jnp.bfloat16), "seq", left)
    total = own
    if recv_r is not None:
        total = total + jnp.where(z >= 1, recv_r.astype(jnp.float32), 0.0)
        total = total + jnp.where(z <= chips - 2, recv_l.astype(jnp.float32), 0.0)
    return total


def shards(
    asking_vectors_matrix,
    matched_keys_matrix,
    carried_vectors_matrix,
    upstream_cotangent,
    w_out,
    panel_entry_offsets,
    rightward_panel_per_entry,
):
    nodes_here = asking_vectors_matrix.shape[1]
    width = asking_vectors_matrix.shape[2]
    n_seq = lax.axis_size("seq")
    nodes = nodes_here * n_seq

    grad_here = upstream_cotangent[0]
    up_mine, up_other, core = chip_gather(grad_here)

    groups = n_seq
    group_width = width // groups
    local_heads = group_width // HD

    def to_groups(values):
        return values.reshape(nodes_here, groups, group_width).transpose(1, 0, 2)

    stacked = jnp.stack(
        [
            to_groups(asking_vectors_matrix[0]),
            to_groups(matched_keys_matrix[0]),
            to_groups(carried_vectors_matrix[0]),
        ]
    )
    heads = lax.all_to_all(stacked, "seq", split_axis=1, concat_axis=1, tiled=True)
    heads = heads.reshape(3, nodes, group_width)

    allowed = tile_mask(panel_entry_offsets[0], rightward_panel_per_entry[0], nodes)

    def head_cols(values, h):
        return values[:, h * HD : (h + 1) * HD]

    fwd = [
        attend(head_cols(heads[0], h), head_cols(heads[1], h), head_cols(heads[2], h), allowed)
        for h in range(local_heads)
    ]
    att_flat = jnp.concatenate([f[0] for f in fwd], axis=1)

    layer_out = chip_layer_out(att_flat, w_out).astype(jnp.bfloat16)[None]

    def times_w(values):
        return lax.dot_general(
            values, w_out, (((2,), (1,)), ((), ())), preferred_element_type=jnp.float32
        ).astype(jnp.bfloat16)

    g_flat = pair_rows(times_w(up_mine), times_w(up_other), core).reshape(nodes, group_width)

    att4 = att_flat.reshape(n_seq // 2, 2, nodes_here, group_width)
    att_mine = jnp.where(core == 0, att4[:, 0], att4[:, 1])
    att_other = jnp.where(core == 0, att4[:, 1], att4[:, 0])

    def block_terms(att_part, up_part):
        return jnp.einsum(
            "bnf,bnk->bfk", att_part, up_part, preferred_element_type=jnp.float32
        ).astype(jnp.bfloat16)

    w_rows = jnp.sum(block_terms(att_mine, up_mine).astype(jnp.float32), axis=0) + jnp.sum(
        block_terms(att_other, up_other).astype(jnp.float32), axis=0
    )
    w_rows = lax.psum(w_rows.astype(jnp.bfloat16), "dp").astype(jnp.float32)
    batch = asking_vectors_matrix.shape[0] * lax.axis_size("dp")
    w_out_grad = w_rows / batch

    bwd = [
        attend_back(
            head_cols(heads[0], h),
            head_cols(heads[1], h),
            head_cols(heads[2], h),
            head_cols(g_flat, h),
            fwd[h][0],
            fwd[h][1],
            fwd[h][2],
        )
        for h in range(local_heads)
    ]
    grads = jnp.stack(
        [jnp.concatenate([b[i] for b in bwd], axis=1).reshape(groups, nodes_here, group_width)
         for i in range(3)]
    )
    back = lax.all_to_all(grads, "seq", split_axis=1, concat_axis=1, tiled=True)
    back = back.transpose(0, 2, 1, 3).reshape(3, 1, nodes_here, width)
    return (layer_out, back[0], back[1], back[2], w_out_grad)


def solution(mesh):
    return jax.shard_map(
        shards,
        mesh=mesh,
        in_specs=(
            P("dp", "seq", None),
            P("dp", "seq", None),
            P("dp", "seq", None),
            P("dp", "seq", None),
            P("seq", None),
            P("dp", None),
            P("dp", None),
        ),
        out_specs=(
            P("dp", "seq", None),
            P("dp", "seq", None),
            P("dp", "seq", None),
            P("dp", "seq", None),
            P("seq", None),
        ),
        check_vma=False,
    )
```

```python
import math

import jax
import jax.numpy as jnp
from jax import lax
from jax.sharding import PartitionSpec as P

H = 16
HD = 128


def tile_mask(starts, columns, nodes):
    tile_count = starts.shape[0] - 1
    slot_count = columns.shape[0]
    tile_size = nodes // tile_count
    slot_index = jnp.arange(slot_count, dtype=jnp.int32)
    entry_row = jnp.sum((starts[1:][None, :] <= slot_index[:, None]).astype(jnp.int32), axis=1)
    tile_ids = jnp.arange(tile_count, dtype=jnp.int32)
    row_hot = (entry_row[:, None] == tile_ids[None, :]).astype(jnp.int32)
    col_hot = (columns[:, None] == tile_ids[None, :]).astype(jnp.int32)
    pairs = jnp.einsum("er,ec->rc", row_hot, col_hot) > 0
    full = jnp.broadcast_to(
        pairs[:, None, :, None], (tile_count, tile_size, tile_count, tile_size)
    )
    return full.reshape(nodes, nodes)


def attend(q, k, v, allowed):
    factor = 1.0 / math.sqrt(q.shape[-1])
    scores = jnp.dot(q, k.T, preferred_element_type=jnp.float32) * factor
    masked = jnp.where(allowed, scores, -jnp.inf)
    row_max = jnp.max(masked, axis=1, keepdims=True)
    expd = jnp.where(allowed, jnp.exp(scores - row_max), 0.0)
    row_total = jnp.sum(expd, axis=1, keepdims=True)
    weighted = jnp.dot(expd.astype(jnp.bfloat16), v, preferred_element_type=jnp.float32)
    attended = (weighted / row_total).astype(jnp.bfloat16)
    return attended, expd, row_total


def attend_back(q, k, v, g, attended, expd, row_total):
    factor = 1.0 / math.sqrt(q.shape[-1])
    prob = expd / row_total
    prob_low = prob.astype(jnp.bfloat16)
    v_grad = jnp.dot(prob_low.T, g, preferred_element_type=jnp.float32)
    prob_grad = jnp.dot(g, v.T, preferred_element_type=jnp.float32)
    delta = jnp.sum(
        attended.astype(jnp.float32) * g.astype(jnp.float32), axis=1, keepdims=True
    )
    score_grad = (prob * (prob_grad - delta) * factor).astype(jnp.bfloat16)
    q_grad = jnp.dot(score_grad, k, preferred_element_type=jnp.float32)
    k_grad = jnp.dot(score_grad.T, q, preferred_element_type=jnp.float32)
    return (
        q_grad.astype(jnp.bfloat16),
        k_grad.astype(jnp.bfloat16),
        v_grad.astype(jnp.bfloat16),
    )


def chip_partial_rows(att_flat, w_out):
    n = lax.axis_size("seq")
    rows = att_flat.shape[0] // n
    chips = n // 2
    s = lax.axis_index("seq")
    core = s % 2
    z = s // 2
    sibling = [(i, i ^ 1) for i in range(n)]
    att_sib = lax.ppermute(att_flat, "seq", sibling)
    w_sib = lax.ppermute(w_out, "seq", sibling)

    def parity_rows(values):
        quads = values.reshape(chips, 2, rows, values.shape[1])
        return jnp.where(core == 0, quads[:, 0], quads[:, 1])

    att_chip = jnp.concatenate([parity_rows(att_flat), parity_rows(att_sib)], axis=2)
    w_chip = jnp.concatenate([w_out, w_sib], axis=0)
    chip_partial = lax.dot_general(
        att_chip, w_chip, (((2,), (0,)), ((), ())), preferred_element_type=jnp.float32
    )
    return chip_partial


def chip_exchange(chip_partial):
    n = lax.axis_size("seq")
    chips = n // 2
    z = lax.axis_index("seq") // 2
    total = lax.dynamic_index_in_dim(chip_partial, z, 0, keepdims=False)
    sent = chip_partial.astype(jnp.bfloat16)
    for k in range(1, chips):
        pairs = [(i, ((i // 2 + k) % chips) * 2 + i % 2) for i in range(n)]
        piece = lax.dynamic_index_in_dim(sent, (z + k) % chips, 0, keepdims=False)
        total = total + lax.ppermute(piece, "seq", pairs).astype(jnp.float32)
    return total


def shards(
    asking_vectors_matrix,
    matched_keys_matrix,
    carried_vectors_matrix,
    upstream_cotangent,
    w_out,
    panel_entry_offsets,
    rightward_panel_per_entry,
):
    nodes_here = asking_vectors_matrix.shape[1]
    width = asking_vectors_matrix.shape[2]
    n_seq = lax.axis_size("seq")
    nodes = nodes_here * n_seq

    grad_here = upstream_cotangent[0]
    grad_full = lax.all_gather(grad_here, "seq", axis=0, tiled=True)

    groups = n_seq
    group_width = width // groups
    local_heads = group_width // HD

    def to_groups(values):
        return values.reshape(nodes_here, groups, group_width).transpose(1, 0, 2)

    stacked = jnp.stack(
        [
            to_groups(asking_vectors_matrix[0]),
            to_groups(matched_keys_matrix[0]),
            to_groups(carried_vectors_matrix[0]),
        ]
    )
    heads = lax.all_to_all(stacked, "seq", split_axis=1, concat_axis=1, tiled=True)
    heads = heads.reshape(3, nodes, group_width)

    allowed = tile_mask(panel_entry_offsets[0], rightward_panel_per_entry[0], nodes)

    def head_cols(values, h):
        return values[:, h * HD : (h + 1) * HD]

    fwd = [
        attend(head_cols(heads[0], h), head_cols(heads[1], h), head_cols(heads[2], h), allowed)
        for h in range(local_heads)
    ]
    att_flat = jnp.concatenate([f[0] for f in fwd], axis=1)

    chip_partial = chip_partial_rows(att_flat, w_out)
    chip_partial, fwd = lax.optimization_barrier((chip_partial, fwd))
    layer_out = chip_exchange(chip_partial).astype(jnp.bfloat16)[None]

    g_flat = lax.dot_general(
        grad_full, w_out, (((1,), (1,)), ((), ())), preferred_element_type=jnp.float32
    ).astype(jnp.bfloat16)
    att_blocks = att_flat.reshape(n_seq, nodes_here, local_heads * HD)
    grad_blocks = grad_full.reshape(n_seq, nodes_here, width)
    terms = jnp.einsum(
        "bnf,bnk->bfk", att_blocks, grad_blocks, preferred_element_type=jnp.float32
    ).astype(jnp.bfloat16)
    w_rows = jnp.sum(terms.astype(jnp.float32), axis=0)
    w_rows = lax.psum(w_rows.astype(jnp.bfloat16), "dp").astype(jnp.float32)
    batch = asking_vectors_matrix.shape[0] * lax.axis_size("dp")
    w_out_grad = w_rows / batch

    bwd = [
        attend_back(
            head_cols(heads[0], h),
            head_cols(heads[1], h),
            head_cols(heads[2], h),
            head_cols(g_flat, h),
            fwd[h][0],
            fwd[h][1],
            fwd[h][2],
        )
        for h in range(local_heads)
    ]
    grads = jnp.stack(
        [jnp.concatenate([b[i] for b in bwd], axis=1).reshape(groups, nodes_here, group_width)
         for i in range(3)]
    )
    back = lax.all_to_all(grads, "seq", split_axis=1, concat_axis=1, tiled=True)
    back = back.transpose(0, 2, 1, 3).reshape(3, 1, nodes_here, width)
    return (layer_out, back[0], back[1], back[2], w_out_grad)


def solution(mesh):
    return jax.shard_map(
        shards,
        mesh=mesh,
        in_specs=(
            P("dp", "seq", None),
            P("dp", "seq", None),
            P("dp", "seq", None),
            P("dp", "seq", None),
            P("seq", None),
            P("dp", None),
            P("dp", None),
        ),
        out_specs=(
            P("dp", "seq", None),
            P("dp", "seq", None),
            P("dp", "seq", None),
            P("dp", "seq", None),
            P("seq", None),
        ),
        check_vma=False,
    )
```

```python
import math

import jax
import jax.numpy as jnp
from jax import lax
from jax.sharding import PartitionSpec as P

H = 16
HD = 128


def tile_mask(starts, columns, nodes):
    tile_count = starts.shape[0] - 1
    slot_count = columns.shape[0]
    tile_size = nodes // tile_count
    slot_index = jnp.arange(slot_count, dtype=jnp.int32)
    entry_row = jnp.sum((starts[1:][None, :] <= slot_index[:, None]).astype(jnp.int32), axis=1)
    tile_ids = jnp.arange(tile_count, dtype=jnp.int32)
    row_hot = (entry_row[:, None] == tile_ids[None, :]).astype(jnp.int32)
    col_hot = (columns[:, None] == tile_ids[None, :]).astype(jnp.int32)
    pairs = jnp.einsum("er,ec->rc", row_hot, col_hot) > 0
    full = jnp.broadcast_to(
        pairs[:, None, :, None], (tile_count, tile_size, tile_count, tile_size)
    )
    return full.reshape(nodes, nodes)


def attend(q, k, v, allowed):
    factor = 1.0 / math.sqrt(q.shape[-1])
    scores = jnp.dot(q, k.T, preferred_element_type=jnp.float32) * factor
    masked = jnp.where(allowed, scores, -jnp.inf)
    row_max = jnp.max(masked, axis=1, keepdims=True)
    expd = jnp.where(allowed, jnp.exp(scores - row_max), 0.0)
    row_total = jnp.sum(expd, axis=1, keepdims=True)
    weighted = jnp.dot(expd.astype(jnp.bfloat16), v, preferred_element_type=jnp.float32)
    attended = (weighted / row_total).astype(jnp.bfloat16)
    return attended, expd, row_total


def attend_back(q, k, v, g, attended, expd, row_total):
    factor = 1.0 / math.sqrt(q.shape[-1])
    prob = expd / row_total
    prob_low = prob.astype(jnp.bfloat16)
    v_grad = jnp.dot(prob_low.T, g, preferred_element_type=jnp.float32)
    prob_grad = jnp.dot(g, v.T, preferred_element_type=jnp.float32)
    delta = jnp.sum(
        attended.astype(jnp.float32) * g.astype(jnp.float32), axis=1, keepdims=True
    )
    score_grad = (prob * (prob_grad - delta) * factor).astype(jnp.bfloat16)
    q_grad = jnp.dot(score_grad, k, preferred_element_type=jnp.float32)
    k_grad = jnp.dot(score_grad.T, q, preferred_element_type=jnp.float32)
    return (
        q_grad.astype(jnp.bfloat16),
        k_grad.astype(jnp.bfloat16),
        v_grad.astype(jnp.bfloat16),
    )


def chip_layer_out(att_flat, w_out):
    n = lax.axis_size("seq")
    rows = att_flat.shape[0] // n
    chips = n // 2
    s = lax.axis_index("seq")
    core = s % 2
    z = s // 2
    sibling = [(i, i ^ 1) for i in range(n)]
    att_sib = lax.ppermute(att_flat, "seq", sibling)
    w_sib = lax.ppermute(w_out, "seq", sibling)

    def parity_rows(values):
        quads = values.reshape(chips, 2, rows, values.shape[1])
        return jnp.where(core == 0, quads[:, 0], quads[:, 1])

    att_chip = jnp.concatenate([parity_rows(att_flat), parity_rows(att_sib)], axis=2)
    w_chip = jnp.concatenate([w_out, w_sib], axis=0)
    chip_partial = lax.dot_general(
        att_chip, w_chip, (((2,), (0,)), ((), ())), preferred_element_type=jnp.float32
    )
    total = lax.dynamic_index_in_dim(chip_partial, z, 0, keepdims=False)
    sent = chip_partial.astype(jnp.bfloat16)
    for k in range(1, chips):
        pairs = [(i, ((i // 2 + k) % chips) * 2 + i % 2) for i in range(n)]
        piece = lax.dynamic_index_in_dim(sent, (z + k) % chips, 0, keepdims=False)
        total = total + lax.ppermute(piece, "seq", pairs).astype(jnp.float32)
    return total


def shards(
    asking_vectors_matrix,
    matched_keys_matrix,
    carried_vectors_matrix,
    upstream_cotangent,
    w_out,
    panel_entry_offsets,
    rightward_panel_per_entry,
):
    nodes_here = asking_vectors_matrix.shape[1]
    width = asking_vectors_matrix.shape[2]
    n_seq = lax.axis_size("seq")
    nodes = nodes_here * n_seq

    grad_here = upstream_cotangent[0]
    grad_full = lax.all_gather(grad_here, "seq", axis=0, tiled=True)

    groups = n_seq
    group_width = width // groups
    local_heads = group_width // HD

    stacked = jnp.stack(
        [asking_vectors_matrix[0], matched_keys_matrix[0], carried_vectors_matrix[0]]
    )
    heads = lax.all_to_all(stacked, "seq", split_axis=2, concat_axis=1, tiled=True)

    allowed = tile_mask(panel_entry_offsets[0], rightward_panel_per_entry[0], nodes)

    def head_cols(values, h):
        return values[:, h * HD : (h + 1) * HD]

    fwd = [
        attend(head_cols(heads[0], h), head_cols(heads[1], h), head_cols(heads[2], h), allowed)
        for h in range(local_heads)
    ]
    att_flat = jnp.concatenate([f[0] for f in fwd], axis=1)

    layer_out = chip_layer_out(att_flat, w_out).astype(jnp.bfloat16)[None]

    g_flat = lax.dot_general(
        grad_full, w_out, (((1,), (1,)), ((), ())), preferred_element_type=jnp.float32
    ).astype(jnp.bfloat16)
    att_blocks = att_flat.reshape(n_seq, nodes_here, local_heads * HD)
    grad_blocks = grad_full.reshape(n_seq, nodes_here, width)
    terms = jnp.einsum(
        "bnf,bnk->bfk", att_blocks, grad_blocks, preferred_element_type=jnp.float32
    ).astype(jnp.bfloat16)
    w_rows = jnp.sum(terms.astype(jnp.float32), axis=0)
    w_rows = lax.psum(w_rows.astype(jnp.bfloat16), "dp").astype(jnp.float32)
    batch = asking_vectors_matrix.shape[0] * lax.axis_size("dp")
    w_out_grad = w_rows / batch

    bwd = [
        attend_back(
            head_cols(heads[0], h),
            head_cols(heads[1], h),
            head_cols(heads[2], h),
            head_cols(g_flat, h),
            fwd[h][0],
            fwd[h][1],
            fwd[h][2],
        )
        for h in range(local_heads)
    ]
    grads = jnp.stack([jnp.concatenate([b[i] for b in bwd], axis=1) for i in range(3)])
    back = lax.all_to_all(grads, "seq", split_axis=1, concat_axis=2, tiled=True)
    back = back.reshape(3, 1, nodes_here, width)
    return (layer_out, back[0], back[1], back[2], w_out_grad)


def solution(mesh):
    return jax.shard_map(
        shards,
        mesh=mesh,
        in_specs=(
            P("dp", "seq", None),
            P("dp", "seq", None),
            P("dp", "seq", None),
            P("dp", "seq", None),
            P("seq", None),
            P("dp", None),
            P("dp", None),
        ),
        out_specs=(
            P("dp", "seq", None),
            P("dp", "seq", None),
            P("dp", "seq", None),
            P("dp", "seq", None),
            P("seq", None),
        ),
        check_vma=False,
    )
```

```python
import math

import jax
import jax.numpy as jnp
from jax import lax
from jax.sharding import PartitionSpec as P

H = 16
HD = 128


def tile_mask(starts, columns, nodes):
    tile_count = starts.shape[0] - 1
    slot_count = columns.shape[0]
    tile_size = nodes // tile_count
    slot_index = jnp.arange(slot_count, dtype=jnp.int32)
    entry_row = jnp.sum((starts[1:][None, :] <= slot_index[:, None]).astype(jnp.int32), axis=1)
    tile_ids = jnp.arange(tile_count, dtype=jnp.int32)
    row_hot = (entry_row[:, None] == tile_ids[None, :]).astype(jnp.int32)
    col_hot = (columns[:, None] == tile_ids[None, :]).astype(jnp.int32)
    pairs = jnp.einsum("er,ec->rc", row_hot, col_hot) > 0
    full = jnp.broadcast_to(
        pairs[:, None, :, None], (tile_count, tile_size, tile_count, tile_size)
    )
    return full.reshape(nodes, nodes)


def attend(q, k, v, allowed):
    factor = 1.0 / math.sqrt(q.shape[-1])
    scores = jnp.dot(q, k.T, preferred_element_type=jnp.float32) * factor
    masked = jnp.where(allowed, scores, -jnp.inf)
    row_max = jnp.max(masked, axis=1, keepdims=True)
    expd = jnp.where(allowed, jnp.exp(scores - row_max), 0.0)
    row_total = jnp.sum(expd, axis=1, keepdims=True)
    weighted = jnp.dot(expd.astype(jnp.bfloat16), v, preferred_element_type=jnp.float32)
    attended = (weighted / row_total).astype(jnp.bfloat16)
    return attended, expd, row_total


def attend_back(q, k, v, g, attended, expd, row_total):
    factor = 1.0 / math.sqrt(q.shape[-1])
    prob = expd / row_total
    prob_low = prob.astype(jnp.bfloat16)
    v_grad = jnp.dot(prob_low.T, g, preferred_element_type=jnp.float32)
    prob_grad = jnp.dot(g, v.T, preferred_element_type=jnp.float32)
    delta = jnp.sum(
        attended.astype(jnp.float32) * g.astype(jnp.float32), axis=1, keepdims=True
    )
    score_grad = (prob * (prob_grad - delta) * factor).astype(jnp.bfloat16)
    q_grad = jnp.dot(score_grad, k, preferred_element_type=jnp.float32)
    k_grad = jnp.dot(score_grad.T, q, preferred_element_type=jnp.float32)
    return (
        q_grad.astype(jnp.bfloat16),
        k_grad.astype(jnp.bfloat16),
        v_grad.astype(jnp.bfloat16),
    )


def chip_layer_out(att_flat, w_out):
    n = lax.axis_size("seq")
    rows = att_flat.shape[0] // n
    chips = n // 2
    s = lax.axis_index("seq")
    core = s % 2
    z = s // 2
    sibling = [(i, i ^ 1) for i in range(n)]
    att_sib = lax.ppermute(att_flat, "seq", sibling)
    w_sib = lax.ppermute(w_out, "seq", sibling)

    def parity_rows(values):
        quads = values.reshape(chips, 2, rows, values.shape[1])
        return jnp.where(core == 0, quads[:, 0], quads[:, 1])

    att_chip = jnp.concatenate([parity_rows(att_flat), parity_rows(att_sib)], axis=2)
    w_chip = jnp.concatenate([w_out, w_sib], axis=0)
    chip_partial = lax.dot_general(
        att_chip, w_chip, (((2,), (0,)), ((), ())), preferred_element_type=jnp.float32
    )
    total = lax.dynamic_index_in_dim(chip_partial, z, 0, keepdims=False)
    sent = chip_partial.astype(jnp.bfloat16)
    for k in range(1, chips):
        pairs = [(i, ((i // 2 + k) % chips) * 2 + i % 2) for i in range(n)]
        piece = lax.dynamic_index_in_dim(sent, (z + k) % chips, 0, keepdims=False)
        total = total + lax.ppermute(piece, "seq", pairs).astype(jnp.float32)
    return total


def shards(
    asking_vectors_matrix,
    matched_keys_matrix,
    carried_vectors_matrix,
    upstream_cotangent,
    w_out,
    panel_entry_offsets,
    rightward_panel_per_entry,
):
    nodes_here = asking_vectors_matrix.shape[1]
    width = asking_vectors_matrix.shape[2]
    n_seq = lax.axis_size("seq")
    nodes = nodes_here * n_seq

    grad_here = upstream_cotangent[0]

    groups = n_seq
    group_width = width // groups
    local_heads = group_width // HD

    def to_groups(values):
        return values.reshape(nodes_here, groups, group_width).transpose(1, 0, 2)

    stacked = jnp.stack(
        [
            to_groups(asking_vectors_matrix[0]),
            to_groups(matched_keys_matrix[0]),
            to_groups(carried_vectors_matrix[0]),
        ]
    )
    heads = lax.all_to_all(stacked, "seq", split_axis=1, concat_axis=1, tiled=True)
    heads = heads.reshape(3, nodes, group_width)
    heads, grad_here = lax.optimization_barrier((heads, grad_here))
    grad_full = lax.all_gather(grad_here, "seq", axis=0, tiled=True)

    allowed = tile_mask(panel_entry_offsets[0], rightward_panel_per_entry[0], nodes)

    def head_cols(values, h):
        return values[:, h * HD : (h + 1) * HD]

    fwd = [
        attend(head_cols(heads[0], h), head_cols(heads[1], h), head_cols(heads[2], h), allowed)
        for h in range(local_heads)
    ]
    att_flat = jnp.concatenate([f[0] for f in fwd], axis=1)

    layer_out = chip_layer_out(att_flat, w_out).astype(jnp.bfloat16)[None]

    g_flat = lax.dot_general(
        grad_full, w_out, (((1,), (1,)), ((), ())), preferred_element_type=jnp.float32
    ).astype(jnp.bfloat16)
    att_blocks = att_flat.reshape(n_seq, nodes_here, local_heads * HD)
    grad_blocks = grad_full.reshape(n_seq, nodes_here, width)
    terms = jnp.einsum(
        "bnf,bnk->bfk", att_blocks, grad_blocks, preferred_element_type=jnp.float32
    ).astype(jnp.bfloat16)
    w_rows = jnp.sum(terms.astype(jnp.float32), axis=0)
    w_rows = lax.psum(w_rows.astype(jnp.bfloat16), "dp").astype(jnp.float32)
    batch = asking_vectors_matrix.shape[0] * lax.axis_size("dp")
    w_out_grad = w_rows / batch

    bwd = [
        attend_back(
            head_cols(heads[0], h),
            head_cols(heads[1], h),
            head_cols(heads[2], h),
            head_cols(g_flat, h),
            fwd[h][0],
            fwd[h][1],
            fwd[h][2],
        )
        for h in range(local_heads)
    ]
    grads = jnp.stack(
        [jnp.concatenate([b[i] for b in bwd], axis=1).reshape(groups, nodes_here, group_width)
         for i in range(3)]
    )
    back = lax.all_to_all(grads, "seq", split_axis=1, concat_axis=1, tiled=True)
    back = back.transpose(0, 2, 1, 3).reshape(3, 1, nodes_here, width)
    return (layer_out, back[0], back[1], back[2], w_out_grad)


def solution(mesh):
    return jax.shard_map(
        shards,
        mesh=mesh,
        in_specs=(
            P("dp", "seq", None),
            P("dp", "seq", None),
            P("dp", "seq", None),
            P("dp", "seq", None),
            P("seq", None),
            P("dp", None),
            P("dp", None),
        ),
        out_specs=(
            P("dp", "seq", None),
            P("dp", "seq", None),
            P("dp", "seq", None),
            P("dp", "seq", None),
            P("seq", None),
        ),
        check_vma=False,
    )
```

```python
import math

import jax
import jax.numpy as jnp
from jax import lax
from jax.sharding import PartitionSpec as P

H = 16
HD = 128


def tile_mask(starts, columns, nodes):
    tile_count = starts.shape[0] - 1
    slot_count = columns.shape[0]
    tile_size = nodes // tile_count
    slot_index = jnp.arange(slot_count, dtype=jnp.int32)
    entry_row = jnp.sum((starts[1:][None, :] <= slot_index[:, None]).astype(jnp.int32), axis=1)
    tile_ids = jnp.arange(tile_count, dtype=jnp.int32)
    row_hot = (entry_row[:, None] == tile_ids[None, :]).astype(jnp.int32)
    col_hot = (columns[:, None] == tile_ids[None, :]).astype(jnp.int32)
    pairs = jnp.einsum("er,ec->rc", row_hot, col_hot) > 0
    full = jnp.broadcast_to(
        pairs[:, None, :, None], (tile_count, tile_size, tile_count, tile_size)
    )
    return full.reshape(nodes, nodes)


def attend(q, k, v, allowed):
    factor = 1.0 / math.sqrt(q.shape[-1])
    scores = jnp.dot(q, k.T, preferred_element_type=jnp.float32) * factor
    masked = jnp.where(allowed, scores, -jnp.inf)
    row_max = jnp.max(masked, axis=1, keepdims=True)
    expd = jnp.where(allowed, jnp.exp(scores - row_max), 0.0)
    row_total = jnp.sum(expd, axis=1, keepdims=True)
    weighted = jnp.dot(expd.astype(jnp.bfloat16), v, preferred_element_type=jnp.float32)
    attended = (weighted / row_total).astype(jnp.bfloat16)
    return attended, expd, row_total


def attend_back(q, k, v, g, attended, expd, row_total):
    factor = 1.0 / math.sqrt(q.shape[-1])
    prob = expd / row_total
    prob_low = prob.astype(jnp.bfloat16)
    v_grad = jnp.dot(prob_low.T, g, preferred_element_type=jnp.float32)
    prob_grad = jnp.dot(g, v.T, preferred_element_type=jnp.float32)
    delta = jnp.sum(
        attended.astype(jnp.float32) * g.astype(jnp.float32), axis=1, keepdims=True
    )
    score_grad = (prob * (prob_grad - delta) * factor).astype(jnp.bfloat16)
    q_grad = jnp.dot(score_grad, k, preferred_element_type=jnp.float32)
    k_grad = jnp.dot(score_grad.T, q, preferred_element_type=jnp.float32)
    return (
        q_grad.astype(jnp.bfloat16),
        k_grad.astype(jnp.bfloat16),
        v_grad.astype(jnp.bfloat16),
    )


def chip_layer_out(att_flat, w_out):
    n = lax.axis_size("seq")
    rows = att_flat.shape[0] // n
    chips = n // 2
    s = lax.axis_index("seq")
    core = s % 2
    z = s // 2
    sibling = [(i, i ^ 1) for i in range(n)]
    att_sib = lax.ppermute(att_flat, "seq", sibling)
    w_sib = lax.ppermute(w_out, "seq", sibling)

    def parity_rows(values):
        quads = values.reshape(chips, 2, rows, values.shape[1])
        return jnp.where(core == 0, quads[:, 0], quads[:, 1])

    att_chip = jnp.concatenate([parity_rows(att_flat), parity_rows(att_sib)], axis=2)
    w_chip = jnp.concatenate([w_out, w_sib], axis=0)
    chip_partial = lax.dot_general(
        att_chip, w_chip, (((2,), (0,)), ((), ())), preferred_element_type=jnp.float32
    )
    total = lax.dynamic_index_in_dim(chip_partial, z, 0, keepdims=False)
    sent = chip_partial.astype(jnp.bfloat16)
    for k in range(1, chips):
        pairs = [(i, ((i // 2 + k) % chips) * 2 + i % 2) for i in range(n)]
        piece = lax.dynamic_index_in_dim(sent, (z + k) % chips, 0, keepdims=False)
        total = total + lax.ppermute(piece, "seq", pairs).astype(jnp.float32)
    return total


def shards(
    asking_vectors_matrix,
    matched_keys_matrix,
    carried_vectors_matrix,
    upstream_cotangent,
    w_out,
    panel_entry_offsets,
    rightward_panel_per_entry,
):
    nodes_here = asking_vectors_matrix.shape[1]
    width = asking_vectors_matrix.shape[2]
    n_seq = lax.axis_size("seq")
    nodes = nodes_here * n_seq

    grad_here = upstream_cotangent[0]
    grad_full = lax.all_gather(grad_here, "seq", axis=0, tiled=True)

    groups = n_seq
    group_width = width // groups
    local_heads = group_width // HD

    def head_chunks(values, h):
        split = values.reshape(nodes_here, groups, local_heads, HD)[:, :, h, :]
        return split.transpose(1, 0, 2)

    per_head = []
    for h in range(local_heads):
        stacked = jnp.stack(
            [
                head_chunks(asking_vectors_matrix[0], h),
                head_chunks(matched_keys_matrix[0], h),
                head_chunks(carried_vectors_matrix[0], h),
            ]
        )
        moved = lax.all_to_all(stacked, "seq", split_axis=1, concat_axis=1, tiled=True)
        per_head.append(moved.reshape(3, nodes, HD))

    allowed = tile_mask(panel_entry_offsets[0], rightward_panel_per_entry[0], nodes)

    def head_cols(values, h):
        return values[:, h * HD : (h + 1) * HD]

    fwd = [
        attend(per_head[h][0], per_head[h][1], per_head[h][2], allowed)
        for h in range(local_heads)
    ]
    att_flat = jnp.concatenate([f[0] for f in fwd], axis=1)

    layer_out = chip_layer_out(att_flat, w_out).astype(jnp.bfloat16)[None]

    g_flat = lax.dot_general(
        grad_full, w_out, (((1,), (1,)), ((), ())), preferred_element_type=jnp.float32
    ).astype(jnp.bfloat16)
    att_blocks = att_flat.reshape(n_seq, nodes_here, local_heads * HD)
    grad_blocks = grad_full.reshape(n_seq, nodes_here, width)
    terms = jnp.einsum(
        "bnf,bnk->bfk", att_blocks, grad_blocks, preferred_element_type=jnp.float32
    ).astype(jnp.bfloat16)
    w_rows = jnp.sum(terms.astype(jnp.float32), axis=0)
    w_rows = lax.psum(w_rows.astype(jnp.bfloat16), "dp").astype(jnp.float32)
    batch = asking_vectors_matrix.shape[0] * lax.axis_size("dp")
    w_out_grad = w_rows / batch

    returned = []
    for h in range(local_heads):
        q_g, k_g, v_g = attend_back(
            per_head[h][0],
            per_head[h][1],
            per_head[h][2],
            head_cols(g_flat, h),
            fwd[h][0],
            fwd[h][1],
            fwd[h][2],
        )
        grads = jnp.stack([q_g, k_g, v_g]).reshape(3, groups, nodes_here, HD)
        returned.append(lax.all_to_all(grads, "seq", split_axis=1, concat_axis=1, tiled=True))
    back = jnp.stack(returned, axis=3).transpose(0, 2, 1, 3, 4).reshape(3, 1, nodes_here, width)
    return (layer_out, back[0], back[1], back[2], w_out_grad)


def solution(mesh):
    return jax.shard_map(
        shards,
        mesh=mesh,
        in_specs=(
            P("dp", "seq", None),
            P("dp", "seq", None),
            P("dp", "seq", None),
            P("dp", "seq", None),
            P("seq", None),
            P("dp", None),
            P("dp", None),
        ),
        out_specs=(
            P("dp", "seq", None),
            P("dp", "seq", None),
            P("dp", "seq", None),
            P("dp", "seq", None),
            P("seq", None),
        ),
        check_vma=False,
    )
```

```python
import math

import jax
import jax.numpy as jnp
from jax import lax
from jax.sharding import PartitionSpec as P

H = 16
HD = 128


def tile_mask(starts, columns, nodes):
    tile_count = starts.shape[0] - 1
    slot_count = columns.shape[0]
    tile_size = nodes // tile_count
    slot_index = jnp.arange(slot_count, dtype=jnp.int32)
    entry_row = jnp.sum((starts[1:][None, :] <= slot_index[:, None]).astype(jnp.int32), axis=1)
    tile_ids = jnp.arange(tile_count, dtype=jnp.int32)
    row_hot = (entry_row[:, None] == tile_ids[None, :]).astype(jnp.int32)
    col_hot = (columns[:, None] == tile_ids[None, :]).astype(jnp.int32)
    pairs = jnp.einsum("er,ec->rc", row_hot, col_hot) > 0
    full = jnp.broadcast_to(
        pairs[:, None, :, None], (tile_count, tile_size, tile_count, tile_size)
    )
    return full.reshape(nodes, nodes)


def attend(q, k, v, allowed):
    factor = 1.0 / math.sqrt(q.shape[-1])
    scores = jnp.dot(q, k.T, preferred_element_type=jnp.float32) * factor
    masked = jnp.where(allowed, scores, -jnp.inf)
    row_max = jnp.max(masked, axis=1, keepdims=True)
    expd = jnp.where(allowed, jnp.exp(scores - row_max), 0.0)
    row_total = jnp.sum(expd, axis=1, keepdims=True)
    weighted = jnp.dot(expd.astype(jnp.bfloat16), v, preferred_element_type=jnp.float32)
    attended = (weighted / row_total).astype(jnp.bfloat16)
    return attended, expd, row_total


def attend_back(q, k, v, g, attended, expd, row_total):
    factor = 1.0 / math.sqrt(q.shape[-1])
    prob = expd / row_total
    prob_low = prob.astype(jnp.bfloat16)
    v_grad = jnp.dot(prob_low.T, g, preferred_element_type=jnp.float32)
    prob_grad = jnp.dot(g, v.T, preferred_element_type=jnp.float32)
    delta = jnp.sum(
        attended.astype(jnp.float32) * g.astype(jnp.float32), axis=1, keepdims=True
    )
    score_grad = (prob * (prob_grad - delta) * factor).astype(jnp.bfloat16)
    q_grad = jnp.dot(score_grad, k, preferred_element_type=jnp.float32)
    k_grad = jnp.dot(score_grad.T, q, preferred_element_type=jnp.float32)
    return (
        q_grad.astype(jnp.bfloat16),
        k_grad.astype(jnp.bfloat16),
        v_grad.astype(jnp.bfloat16),
    )


def chip_layer_out(att_flat, w_out):
    n = lax.axis_size("seq")
    rows = att_flat.shape[0] // n
    chips = n // 2
    s = lax.axis_index("seq")
    core = s % 2
    z = s // 2
    sibling = [(i, i ^ 1) for i in range(n)]
    att_sib = lax.ppermute(att_flat, "seq", sibling)
    w_sib = lax.ppermute(w_out, "seq", sibling)

    def parity_rows(values):
        quads = values.reshape(chips, 2, rows, values.shape[1])
        return jnp.where(core == 0, quads[:, 0], quads[:, 1])

    att_chip = jnp.concatenate([parity_rows(att_flat), parity_rows(att_sib)], axis=2)
    w_chip = jnp.concatenate([w_out, w_sib], axis=0)
    chip_partial = lax.dot_general(
        att_chip, w_chip, (((2,), (0,)), ((), ())), preferred_element_type=jnp.float32
    )
    total = lax.dynamic_index_in_dim(chip_partial, z, 0, keepdims=False)
    sent = chip_partial.astype(jnp.bfloat16)
    moved = []
    for k in range(1, chips):
        pairs = [(i, ((i // 2 + k) % chips) * 2 + i % 2) for i in range(n)]
        piece = lax.dynamic_index_in_dim(sent, (z + k) % chips, 0, keepdims=False)
        moved.append(lax.ppermute(piece, "seq", pairs))
    for piece in moved:
        total = total + piece.astype(jnp.float32)
    return total, sent


def shards(
    asking_vectors_matrix,
    matched_keys_matrix,
    carried_vectors_matrix,
    upstream_cotangent,
    w_out,
    panel_entry_offsets,
    rightward_panel_per_entry,
):
    nodes_here = asking_vectors_matrix.shape[1]
    width = asking_vectors_matrix.shape[2]
    n_seq = lax.axis_size("seq")
    nodes = nodes_here * n_seq

    grad_here = upstream_cotangent[0]
    grad_full = lax.all_gather(grad_here, "seq", axis=0, tiled=True)

    groups = n_seq
    group_width = width // groups
    local_heads = group_width // HD

    def to_groups(values):
        return values.reshape(nodes_here, groups, group_width).transpose(1, 0, 2)

    stacked = jnp.stack(
        [
            to_groups(asking_vectors_matrix[0]),
            to_groups(matched_keys_matrix[0]),
            to_groups(carried_vectors_matrix[0]),
        ]
    )
    heads = lax.all_to_all(stacked, "seq", split_axis=1, concat_axis=1, tiled=True)
    heads = heads.reshape(3, nodes, group_width)

    allowed = tile_mask(panel_entry_offsets[0], rightward_panel_per_entry[0], nodes)

    def head_cols(values, h):
        return values[:, h * HD : (h + 1) * HD]

    fwd = [
        attend(head_cols(heads[0], h), head_cols(heads[1], h), head_cols(heads[2], h), allowed)
        for h in range(local_heads)
    ]
    att_flat = jnp.concatenate([f[0] for f in fwd], axis=1)

    layer_total, sent = chip_layer_out(att_flat, w_out)
    layer_out = layer_total.astype(jnp.bfloat16)[None]
    sent, att_later, grad_later = lax.optimization_barrier((sent, att_flat, grad_full))

    g_flat = lax.dot_general(
        grad_full, w_out, (((1,), (1,)), ((), ())), preferred_element_type=jnp.float32
    ).astype(jnp.bfloat16)
    att_blocks = att_later.reshape(n_seq, nodes_here, local_heads * HD)
    grad_blocks = grad_later.reshape(n_seq, nodes_here, width)
    terms = jnp.einsum(
        "bnf,bnk->bfk", att_blocks, grad_blocks, preferred_element_type=jnp.float32
    ).astype(jnp.bfloat16)
    w_rows = jnp.sum(terms.astype(jnp.float32), axis=0)
    w_rows = lax.psum(w_rows.astype(jnp.bfloat16), "dp").astype(jnp.float32)
    batch = asking_vectors_matrix.shape[0] * lax.axis_size("dp")
    w_out_grad = w_rows / batch

    bwd = [
        attend_back(
            head_cols(heads[0], h),
            head_cols(heads[1], h),
            head_cols(heads[2], h),
            head_cols(g_flat, h),
            fwd[h][0],
            fwd[h][1],
            fwd[h][2],
        )
        for h in range(local_heads)
    ]
    grads = jnp.stack(
        [jnp.concatenate([b[i] for b in bwd], axis=1).reshape(groups, nodes_here, group_width)
         for i in range(3)]
    )
    back = lax.all_to_all(grads, "seq", split_axis=1, concat_axis=1, tiled=True)
    back = back.transpose(0, 2, 1, 3).reshape(3, 1, nodes_here, width)
    return (layer_out, back[0], back[1], back[2], w_out_grad)


def solution(mesh):
    return jax.shard_map(
        shards,
        mesh=mesh,
        in_specs=(
            P("dp", "seq", None),
            P("dp", "seq", None),
            P("dp", "seq", None),
            P("dp", "seq", None),
            P("seq", None),
            P("dp", None),
            P("dp", None),
        ),
        out_specs=(
            P("dp", "seq", None),
            P("dp", "seq", None),
            P("dp", "seq", None),
            P("dp", "seq", None),
            P("seq", None),
        ),
        check_vma=False,
    )
```

```python
import math

import jax
import jax.numpy as jnp
from jax import lax
from jax.sharding import PartitionSpec as P

H = 16
HD = 128


def tile_mask(starts, columns, nodes):
    tile_count = starts.shape[0] - 1
    slot_count = columns.shape[0]
    tile_size = nodes // tile_count
    slot_index = jnp.arange(slot_count, dtype=jnp.int32)
    entry_row = jnp.sum((starts[1:][None, :] <= slot_index[:, None]).astype(jnp.int32), axis=1)
    tile_ids = jnp.arange(tile_count, dtype=jnp.int32)
    row_hot = (entry_row[:, None] == tile_ids[None, :]).astype(jnp.int32)
    col_hot = (columns[:, None] == tile_ids[None, :]).astype(jnp.int32)
    pairs = jnp.einsum("er,ec->rc", row_hot, col_hot) > 0
    full = jnp.broadcast_to(
        pairs[:, None, :, None], (tile_count, tile_size, tile_count, tile_size)
    )
    return full.reshape(nodes, nodes)


def attend(q, k, v, allowed):
    factor = 1.0 / math.sqrt(q.shape[-1])
    scores = jnp.dot(q, k.T, preferred_element_type=jnp.float32) * factor
    masked = jnp.where(allowed, scores, -jnp.inf)
    row_max = jnp.max(masked, axis=1, keepdims=True)
    expd = jnp.where(allowed, jnp.exp(scores - row_max), 0.0)
    row_total = jnp.sum(expd, axis=1, keepdims=True)
    weighted = jnp.dot(expd.astype(jnp.bfloat16), v, preferred_element_type=jnp.float32)
    attended = (weighted / row_total).astype(jnp.bfloat16)
    return attended, expd, row_total


def attend_back(q, k, v, g, attended, expd, row_total):
    factor = 1.0 / math.sqrt(q.shape[-1])
    prob = expd / row_total
    prob_low = prob.astype(jnp.bfloat16)
    v_grad = jnp.dot(prob_low.T, g, preferred_element_type=jnp.float32)
    prob_grad = jnp.dot(g, v.T, preferred_element_type=jnp.float32)
    delta = jnp.sum(
        attended.astype(jnp.float32) * g.astype(jnp.float32), axis=1, keepdims=True
    )
    score_grad = (prob * (prob_grad - delta) * factor).astype(jnp.bfloat16)
    q_grad = jnp.dot(score_grad, k, preferred_element_type=jnp.float32)
    k_grad = jnp.dot(score_grad.T, q, preferred_element_type=jnp.float32)
    return (
        q_grad.astype(jnp.bfloat16),
        k_grad.astype(jnp.bfloat16),
        v_grad.astype(jnp.bfloat16),
    )


def chip_layer_out(att_flat, w_out):
    n = lax.axis_size("seq")
    rows = att_flat.shape[0] // n
    chips = n // 2
    s = lax.axis_index("seq")
    core = s % 2
    z = s // 2
    sibling = [(i, i ^ 1) for i in range(n)]
    att_sib = lax.ppermute(att_flat, "seq", sibling)
    w_sib = lax.ppermute(w_out, "seq", sibling)

    def parity_rows(values):
        quads = values.reshape(chips, 2, rows, values.shape[1])
        return jnp.where(core == 0, quads[:, 0], quads[:, 1])

    att_chip = jnp.concatenate([parity_rows(att_flat), parity_rows(att_sib)], axis=2)
    w_chip = jnp.concatenate([w_out, w_sib], axis=0)
    chip_partial = lax.dot_general(
        att_chip, w_chip, (((2,), (0,)), ((), ())), preferred_element_type=jnp.float32
    )
    total = lax.dynamic_index_in_dim(chip_partial, z, 0, keepdims=False)
    sent = chip_partial.astype(jnp.bfloat16)
    for k in range(1, chips):
        pairs = [(i, ((i // 2 + k) % chips) * 2 + i % 2) for i in range(n)]
        piece = lax.dynamic_index_in_dim(sent, (z + k) % chips, 0, keepdims=False)
        total = total + lax.ppermute(piece, "seq", pairs).astype(jnp.float32)
    return total


def shards(
    asking_vectors_matrix,
    matched_keys_matrix,
    carried_vectors_matrix,
    upstream_cotangent,
    w_out,
    panel_entry_offsets,
    rightward_panel_per_entry,
):
    nodes_here = asking_vectors_matrix.shape[1]
    width = asking_vectors_matrix.shape[2]
    n_seq = lax.axis_size("seq")
    nodes = nodes_here * n_seq

    grad_here = upstream_cotangent[0]
    grad_full = lax.all_gather(grad_here, "seq", axis=0, tiled=True)

    groups = n_seq
    group_width = width // groups
    local_heads = group_width // HD

    stacked = (
        jnp.stack([asking_vectors_matrix[0], matched_keys_matrix[0], carried_vectors_matrix[0]])
        .reshape(3, nodes_here, groups, group_width)
        .transpose(0, 2, 1, 3)
    )
    heads = lax.all_to_all(stacked, "seq", split_axis=1, concat_axis=1, tiled=True)
    heads = heads.reshape(3, nodes, group_width)

    allowed = tile_mask(panel_entry_offsets[0], rightward_panel_per_entry[0], nodes)

    def head_cols(values, h):
        return values[:, h * HD : (h + 1) * HD]

    fwd = [
        attend(head_cols(heads[0], h), head_cols(heads[1], h), head_cols(heads[2], h), allowed)
        for h in range(local_heads)
    ]
    att_flat = jnp.concatenate([f[0] for f in fwd], axis=1)

    layer_out = chip_layer_out(att_flat, w_out).astype(jnp.bfloat16)[None]

    g_flat = lax.dot_general(
        grad_full, w_out, (((1,), (1,)), ((), ())), preferred_element_type=jnp.float32
    ).astype(jnp.bfloat16)
    att_blocks = att_flat.reshape(n_seq, nodes_here, local_heads * HD)
    grad_blocks = grad_full.reshape(n_seq, nodes_here, width)
    terms = jnp.einsum(
        "bnf,bnk->bfk", att_blocks, grad_blocks, preferred_element_type=jnp.float32
    ).astype(jnp.bfloat16)
    w_rows = jnp.sum(terms.astype(jnp.float32), axis=0)
    w_rows = lax.psum(w_rows.astype(jnp.bfloat16), "dp").astype(jnp.float32)
    batch = asking_vectors_matrix.shape[0] * lax.axis_size("dp")
    w_out_grad = w_rows / batch

    bwd = [
        attend_back(
            head_cols(heads[0], h),
            head_cols(heads[1], h),
            head_cols(heads[2], h),
            head_cols(g_flat, h),
            fwd[h][0],
            fwd[h][1],
            fwd[h][2],
        )
        for h in range(local_heads)
    ]
    grads = jnp.stack(
        [jnp.concatenate([b[i] for b in bwd], axis=1).reshape(groups, nodes_here, group_width)
         for i in range(3)]
    )
    back = lax.all_to_all(grads, "seq", split_axis=1, concat_axis=1, tiled=True)
    back = back.transpose(0, 2, 1, 3).reshape(3, 1, nodes_here, width)
    return (layer_out, back[0], back[1], back[2], w_out_grad)


def solution(mesh):
    return jax.shard_map(
        shards,
        mesh=mesh,
        in_specs=(
            P("dp", "seq", None),
            P("dp", "seq", None),
            P("dp", "seq", None),
            P("dp", "seq", None),
            P("seq", None),
            P("dp", None),
            P("dp", None),
        ),
        out_specs=(
            P("dp", "seq", None),
            P("dp", "seq", None),
            P("dp", "seq", None),
            P("dp", "seq", None),
            P("seq", None),
        ),
        check_vma=False,
    )
```

```python
import math

import jax
import jax.numpy as jnp
from jax import lax
from jax.sharding import PartitionSpec as P

H = 16
HD = 128


def tile_mask(starts, columns, nodes):
    tile_count = starts.shape[0] - 1
    slot_count = columns.shape[0]
    tile_size = nodes // tile_count
    slot_index = jnp.arange(slot_count, dtype=jnp.int32)
    entry_row = jnp.sum((starts[1:][None, :] <= slot_index[:, None]).astype(jnp.int32), axis=1)
    tile_ids = jnp.arange(tile_count, dtype=jnp.int32)
    row_hot = (entry_row[:, None] == tile_ids[None, :]).astype(jnp.int32)
    col_hot = (columns[:, None] == tile_ids[None, :]).astype(jnp.int32)
    pairs = jnp.einsum("er,ec->rc", row_hot, col_hot) > 0
    full = jnp.broadcast_to(
        pairs[:, None, :, None], (tile_count, tile_size, tile_count, tile_size)
    )
    return full.reshape(nodes, nodes)


def attend(q, k, v, allowed):
    factor = 1.0 / math.sqrt(q.shape[-1])
    scores = jnp.dot(q, k.T, preferred_element_type=jnp.float32) * factor
    masked = jnp.where(allowed, scores, -jnp.inf)
    row_max = jnp.max(masked, axis=1, keepdims=True)
    expd = jnp.exp(masked - row_max)
    row_total = jnp.sum(expd, axis=1, keepdims=True)
    weighted = jnp.dot(expd.astype(jnp.bfloat16), v, preferred_element_type=jnp.float32)
    attended = (weighted / row_total).astype(jnp.bfloat16)
    return attended, expd, row_total


def attend_back(q, k, v, g, attended, expd, row_total):
    factor = 1.0 / math.sqrt(q.shape[-1])
    prob = expd / row_total
    prob_low = prob.astype(jnp.bfloat16)
    v_grad = jnp.dot(prob_low.T, g, preferred_element_type=jnp.float32)
    prob_grad = jnp.dot(g, v.T, preferred_element_type=jnp.float32)
    delta = jnp.sum(
        attended.astype(jnp.float32) * g.astype(jnp.float32), axis=1, keepdims=True
    )
    score_grad = (prob * (prob_grad - delta) * factor).astype(jnp.bfloat16)
    q_grad = jnp.dot(score_grad, k, preferred_element_type=jnp.float32)
    k_grad = jnp.dot(score_grad.T, q, preferred_element_type=jnp.float32)
    return (
        q_grad.astype(jnp.bfloat16),
        k_grad.astype(jnp.bfloat16),
        v_grad.astype(jnp.bfloat16),
    )


def chip_layer_out(att_flat, w_out):
    n = lax.axis_size("seq")
    rows = att_flat.shape[0] // n
    chips = n // 2
    s = lax.axis_index("seq")
    core = s % 2
    z = s // 2
    sibling = [(i, i ^ 1) for i in range(n)]
    att_sib = lax.ppermute(att_flat, "seq", sibling)
    w_sib = lax.ppermute(w_out, "seq", sibling)

    def parity_rows(values):
        quads = values.reshape(chips, 2, rows, values.shape[1])
        return jnp.where(core == 0, quads[:, 0], quads[:, 1])

    att_chip = jnp.concatenate([parity_rows(att_flat), parity_rows(att_sib)], axis=2)
    w_chip = jnp.concatenate([w_out, w_sib], axis=0)
    chip_partial = lax.dot_general(
        att_chip, w_chip, (((2,), (0,)), ((), ())), preferred_element_type=jnp.float32
    )
    total = lax.dynamic_index_in_dim(chip_partial, z, 0, keepdims=False)
    sent = chip_partial.astype(jnp.bfloat16)
    for k in range(1, chips):
        pairs = [(i, ((i // 2 + k) % chips) * 2 + i % 2) for i in range(n)]
        piece = lax.dynamic_index_in_dim(sent, (z + k) % chips, 0, keepdims=False)
        total = total + lax.ppermute(piece, "seq", pairs).astype(jnp.float32)
    return total


def shards(
    asking_vectors_matrix,
    matched_keys_matrix,
    carried_vectors_matrix,
    upstream_cotangent,
    w_out,
    panel_entry_offsets,
    rightward_panel_per_entry,
):
    nodes_here = asking_vectors_matrix.shape[1]
    width = asking_vectors_matrix.shape[2]
    n_seq = lax.axis_size("seq")
    nodes = nodes_here * n_seq

    grad_here = upstream_cotangent[0]
    grad_full = lax.all_gather(grad_here, "seq", axis=0, tiled=True)

    groups = n_seq
    group_width = width // groups
    local_heads = group_width // HD

    def to_groups(values):
        return values.reshape(nodes_here, groups, group_width).transpose(1, 0, 2)

    stacked = jnp.stack(
        [
            to_groups(asking_vectors_matrix[0]),
            to_groups(matched_keys_matrix[0]),
            to_groups(carried_vectors_matrix[0]),
        ]
    )
    heads = lax.all_to_all(stacked, "seq", split_axis=1, concat_axis=1, tiled=True)
    heads = heads.reshape(3, nodes, group_width)

    allowed = tile_mask(panel_entry_offsets[0], rightward_panel_per_entry[0], nodes)

    def head_cols(values, h):
        return values[:, h * HD : (h + 1) * HD]

    fwd = [
        attend(head_cols(heads[0], h), head_cols(heads[1], h), head_cols(heads[2], h), allowed)
        for h in range(local_heads)
    ]
    att_flat = jnp.concatenate([f[0] for f in fwd], axis=1)

    layer_out = chip_layer_out(att_flat, w_out).astype(jnp.bfloat16)[None]

    g_flat = lax.dot_general(
        grad_full, w_out, (((1,), (1,)), ((), ())), preferred_element_type=jnp.float32
    ).astype(jnp.bfloat16)
    att_blocks = att_flat.reshape(n_seq, nodes_here, local_heads * HD)
    grad_blocks = grad_full.reshape(n_seq, nodes_here, width)
    terms = jnp.einsum(
        "bnf,bnk->bfk", att_blocks, grad_blocks, preferred_element_type=jnp.float32
    ).astype(jnp.bfloat16)
    w_rows = jnp.sum(terms.astype(jnp.float32), axis=0)
    w_rows = lax.psum(w_rows.astype(jnp.bfloat16), "dp").astype(jnp.float32)
    batch = asking_vectors_matrix.shape[0] * lax.axis_size("dp")
    w_out_grad = w_rows / batch

    bwd = [
        attend_back(
            head_cols(heads[0], h),
            head_cols(heads[1], h),
            head_cols(heads[2], h),
            head_cols(g_flat, h),
            fwd[h][0],
            fwd[h][1],
            fwd[h][2],
        )
        for h in range(local_heads)
    ]
    grads = jnp.stack(
        [jnp.concatenate([b[i] for b in bwd], axis=1).reshape(groups, nodes_here, group_width)
         for i in range(3)]
    )
    back = lax.all_to_all(grads, "seq", split_axis=1, concat_axis=1, tiled=True)
    back = back.transpose(0, 2, 1, 3).reshape(3, 1, nodes_here, width)
    return (layer_out, back[0], back[1], back[2], w_out_grad)


def solution(mesh):
    return jax.shard_map(
        shards,
        mesh=mesh,
        in_specs=(
            P("dp", "seq", None),
            P("dp", "seq", None),
            P("dp", "seq", None),
            P("dp", "seq", None),
            P("seq", None),
            P("dp", None),
            P("dp", None),
        ),
        out_specs=(
            P("dp", "seq", None),
            P("dp", "seq", None),
            P("dp", "seq", None),
            P("dp", "seq", None),
            P("seq", None),
        ),
        check_vma=False,
    )
```

```python
import math

import jax
import jax.numpy as jnp
from jax import lax
from jax.sharding import PartitionSpec as P

H = 16
HD = 128


def tile_mask(starts, columns, nodes):
    tile_count = starts.shape[0] - 1
    slot_count = columns.shape[0]
    tile_size = nodes // tile_count
    slot_index = jnp.arange(slot_count, dtype=jnp.int32)
    entry_row = jnp.sum((starts[1:][None, :] <= slot_index[:, None]).astype(jnp.int32), axis=1)
    tile_ids = jnp.arange(tile_count, dtype=jnp.int32)
    row_hot = (entry_row[:, None] == tile_ids[None, :]).astype(jnp.int32)
    col_hot = (columns[:, None] == tile_ids[None, :]).astype(jnp.int32)
    pairs = jnp.einsum("er,ec->rc", row_hot, col_hot) > 0
    full = jnp.broadcast_to(
        pairs[:, None, :, None], (tile_count, tile_size, tile_count, tile_size)
    )
    return jnp.where(full.reshape(nodes, nodes), 0.0, -jnp.inf)


def attend(q, k, v, allowed):
    factor = 1.0 / math.sqrt(q.shape[-1])
    scores = jnp.dot(q, k.T, preferred_element_type=jnp.float32) * factor
    masked = scores + allowed
    row_max = jnp.max(masked, axis=1, keepdims=True)
    expd = jnp.exp(masked - row_max)
    row_total = jnp.sum(expd, axis=1, keepdims=True)
    weighted = jnp.dot(expd.astype(jnp.bfloat16), v, preferred_element_type=jnp.float32)
    attended = (weighted / row_total).astype(jnp.bfloat16)
    return attended, expd, row_total


def attend_back(q, k, v, g, attended, expd, row_total):
    factor = 1.0 / math.sqrt(q.shape[-1])
    prob = expd / row_total
    prob_low = prob.astype(jnp.bfloat16)
    v_grad = jnp.dot(prob_low.T, g, preferred_element_type=jnp.float32)
    prob_grad = jnp.dot(g, v.T, preferred_element_type=jnp.float32)
    delta = jnp.sum(
        attended.astype(jnp.float32) * g.astype(jnp.float32), axis=1, keepdims=True
    )
    score_grad = (prob * (prob_grad - delta) * factor).astype(jnp.bfloat16)
    q_grad = jnp.dot(score_grad, k, preferred_element_type=jnp.float32)
    k_grad = jnp.dot(score_grad.T, q, preferred_element_type=jnp.float32)
    return (
        q_grad.astype(jnp.bfloat16),
        k_grad.astype(jnp.bfloat16),
        v_grad.astype(jnp.bfloat16),
    )


def chip_layer_out(att_flat, w_out):
    n = lax.axis_size("seq")
    rows = att_flat.shape[0] // n
    chips = n // 2
    s = lax.axis_index("seq")
    core = s % 2
    z = s // 2
    sibling = [(i, i ^ 1) for i in range(n)]
    att_sib = lax.ppermute(att_flat, "seq", sibling)
    w_sib = lax.ppermute(w_out, "seq", sibling)

    def parity_rows(values):
        quads = values.reshape(chips, 2, rows, values.shape[1])
        return jnp.where(core == 0, quads[:, 0], quads[:, 1])

    att_chip = jnp.concatenate([parity_rows(att_flat), parity_rows(att_sib)], axis=2)
    w_chip = jnp.concatenate([w_out, w_sib], axis=0)
    chip_partial = lax.dot_general(
        att_chip, w_chip, (((2,), (0,)), ((), ())), preferred_element_type=jnp.float32
    )
    total = lax.dynamic_index_in_dim(chip_partial, z, 0, keepdims=False)
    sent = chip_partial.astype(jnp.bfloat16)
    for k in range(1, chips):
        pairs = [(i, ((i // 2 + k) % chips) * 2 + i % 2) for i in range(n)]
        piece = lax.dynamic_index_in_dim(sent, (z + k) % chips, 0, keepdims=False)
        total = total + lax.ppermute(piece, "seq", pairs).astype(jnp.float32)
    return total


def shards(
    asking_vectors_matrix,
    matched_keys_matrix,
    carried_vectors_matrix,
    upstream_cotangent,
    w_out,
    panel_entry_offsets,
    rightward_panel_per_entry,
):
    nodes_here = asking_vectors_matrix.shape[1]
    width = asking_vectors_matrix.shape[2]
    n_seq = lax.axis_size("seq")
    nodes = nodes_here * n_seq

    grad_here = upstream_cotangent[0]
    grad_full = lax.all_gather(grad_here, "seq", axis=0, tiled=True)

    groups = n_seq
    group_width = width // groups
    local_heads = group_width // HD

    def to_groups(values):
        return values.reshape(nodes_here, groups, group_width).transpose(1, 0, 2)

    stacked = jnp.stack(
        [
            to_groups(asking_vectors_matrix[0]),
            to_groups(matched_keys_matrix[0]),
            to_groups(carried_vectors_matrix[0]),
        ]
    )
    heads = lax.all_to_all(stacked, "seq", split_axis=1, concat_axis=1, tiled=True)
    heads = heads.reshape(3, nodes, group_width)

    allowed = tile_mask(panel_entry_offsets[0], rightward_panel_per_entry[0], nodes)

    def head_cols(values, h):
        return values[:, h * HD : (h + 1) * HD]

    fwd = [
        attend(head_cols(heads[0], h), head_cols(heads[1], h), head_cols(heads[2], h), allowed)
        for h in range(local_heads)
    ]
    att_flat = jnp.concatenate([f[0] for f in fwd], axis=1)

    layer_out = chip_layer_out(att_flat, w_out).astype(jnp.bfloat16)[None]

    g_flat = lax.dot_general(
        grad_full, w_out, (((1,), (1,)), ((), ())), preferred_element_type=jnp.float32
    ).astype(jnp.bfloat16)
    att_blocks = att_flat.reshape(n_seq, nodes_here, local_heads * HD)
    grad_blocks = grad_full.reshape(n_seq, nodes_here, width)
    terms = jnp.einsum(
        "bnf,bnk->bfk", att_blocks, grad_blocks, preferred_element_type=jnp.float32
    ).astype(jnp.bfloat16)
    w_rows = jnp.sum(terms.astype(jnp.float32), axis=0)
    w_rows = lax.psum(w_rows.astype(jnp.bfloat16), "dp").astype(jnp.float32)
    batch = asking_vectors_matrix.shape[0] * lax.axis_size("dp")
    w_out_grad = w_rows / batch

    bwd = [
        attend_back(
            head_cols(heads[0], h),
            head_cols(heads[1], h),
            head_cols(heads[2], h),
            head_cols(g_flat, h),
            fwd[h][0],
            fwd[h][1],
            fwd[h][2],
        )
        for h in range(local_heads)
    ]
    grads = jnp.stack(
        [jnp.concatenate([b[i] for b in bwd], axis=1).reshape(groups, nodes_here, group_width)
         for i in range(3)]
    )
    back = lax.all_to_all(grads, "seq", split_axis=1, concat_axis=1, tiled=True)
    back = back.transpose(0, 2, 1, 3).reshape(3, 1, nodes_here, width)
    return (layer_out, back[0], back[1], back[2], w_out_grad)


def solution(mesh):
    return jax.shard_map(
        shards,
        mesh=mesh,
        in_specs=(
            P("dp", "seq", None),
            P("dp", "seq", None),
            P("dp", "seq", None),
            P("dp", "seq", None),
            P("seq", None),
            P("dp", None),
            P("dp", None),
        ),
        out_specs=(
            P("dp", "seq", None),
            P("dp", "seq", None),
            P("dp", "seq", None),
            P("dp", "seq", None),
            P("seq", None),
        ),
        check_vma=False,
    )
```

```python
import math

import jax
import jax.numpy as jnp
from jax import lax
from jax.sharding import PartitionSpec as P

H = 16
HD = 128


def tile_mask(starts, columns, nodes):
    tile_count = starts.shape[0] - 1
    slot_count = columns.shape[0]
    tile_size = nodes // tile_count
    slot_index = jnp.arange(slot_count, dtype=jnp.int32)
    entry_row = jnp.sum((starts[1:][None, :] <= slot_index[:, None]).astype(jnp.int32), axis=1)
    tile_ids = jnp.arange(tile_count, dtype=jnp.int32)
    row_hot = (entry_row[:, None] == tile_ids[None, :]).astype(jnp.int32)
    col_hot = (columns[:, None] == tile_ids[None, :]).astype(jnp.int32)
    pairs = jnp.einsum("er,ec->rc", row_hot, col_hot) > 0
    full = jnp.broadcast_to(
        pairs[:, None, :, None], (tile_count, tile_size, tile_count, tile_size)
    )
    return jnp.where(full.reshape(nodes, nodes), 0.0, -jnp.inf)


def attend(q, k, v, allowed):
    factor = 1.0 / math.sqrt(q.shape[-1])
    scores = jnp.dot(q, k.T, preferred_element_type=jnp.float32) * factor
    masked = scores + allowed
    row_max = jnp.max(masked, axis=1, keepdims=True)
    expd = jnp.exp(masked - row_max)
    row_total = jnp.sum(expd, axis=1, keepdims=True)
    weighted = jnp.dot(expd.astype(jnp.bfloat16), v, preferred_element_type=jnp.float32)
    attended = (weighted / row_total).astype(jnp.bfloat16)
    return attended, expd, row_total


def attend_back(q, k, v, g, attended, expd, row_total):
    factor = 1.0 / math.sqrt(q.shape[-1])
    prob = expd * (1.0 / row_total)
    prob_low = prob.astype(jnp.bfloat16)
    v_grad = jnp.dot(prob_low.T, g, preferred_element_type=jnp.float32)
    prob_grad = jnp.dot(g, v.T, preferred_element_type=jnp.float32)
    delta = jnp.sum(
        attended.astype(jnp.float32) * g.astype(jnp.float32), axis=1, keepdims=True
    )
    score_grad = (prob * (prob_grad - delta) * factor).astype(jnp.bfloat16)
    q_grad = jnp.dot(score_grad, k, preferred_element_type=jnp.float32)
    k_grad = jnp.dot(score_grad.T, q, preferred_element_type=jnp.float32)
    return (
        q_grad.astype(jnp.bfloat16),
        k_grad.astype(jnp.bfloat16),
        v_grad.astype(jnp.bfloat16),
    )


def chip_layer_out(att_flat, w_out):
    n = lax.axis_size("seq")
    rows = att_flat.shape[0] // n
    chips = n // 2
    s = lax.axis_index("seq")
    core = s % 2
    z = s // 2
    sibling = [(i, i ^ 1) for i in range(n)]
    att_sib = lax.ppermute(att_flat, "seq", sibling)
    w_sib = lax.ppermute(w_out, "seq", sibling)

    def parity_rows(values):
        quads = values.reshape(chips, 2, rows, values.shape[1])
        return jnp.where(core == 0, quads[:, 0], quads[:, 1])

    att_chip = jnp.concatenate([parity_rows(att_flat), parity_rows(att_sib)], axis=2)
    w_chip = jnp.concatenate([w_out, w_sib], axis=0)
    chip_partial = lax.dot_general(
        att_chip, w_chip, (((2,), (0,)), ((), ())), preferred_element_type=jnp.float32
    )
    total = lax.dynamic_index_in_dim(chip_partial, z, 0, keepdims=False)
    sent = chip_partial.astype(jnp.bfloat16)
    for k in range(1, chips):
        pairs = [(i, ((i // 2 + k) % chips) * 2 + i % 2) for i in range(n)]
        piece = lax.dynamic_index_in_dim(sent, (z + k) % chips, 0, keepdims=False)
        total = total + lax.ppermute(piece, "seq", pairs).astype(jnp.float32)
    return total


def shards(
    asking_vectors_matrix,
    matched_keys_matrix,
    carried_vectors_matrix,
    upstream_cotangent,
    w_out,
    panel_entry_offsets,
    rightward_panel_per_entry,
):
    nodes_here = asking_vectors_matrix.shape[1]
    width = asking_vectors_matrix.shape[2]
    n_seq = lax.axis_size("seq")
    nodes = nodes_here * n_seq

    grad_here = upstream_cotangent[0]
    grad_full = lax.all_gather(grad_here, "seq", axis=0, tiled=True)

    groups = n_seq
    group_width = width // groups
    local_heads = group_width // HD

    def to_groups(values):
        return values.reshape(nodes_here, groups, group_width).transpose(1, 0, 2)

    stacked = jnp.stack(
        [
            to_groups(asking_vectors_matrix[0]),
            to_groups(matched_keys_matrix[0]),
            to_groups(carried_vectors_matrix[0]),
        ]
    )
    heads = lax.all_to_all(stacked, "seq", split_axis=1, concat_axis=1, tiled=True)
    heads = heads.reshape(3, nodes, group_width)

    allowed = tile_mask(panel_entry_offsets[0], rightward_panel_per_entry[0], nodes)

    def head_cols(values, h):
        return values[:, h * HD : (h + 1) * HD]

    fwd = [
        attend(head_cols(heads[0], h), head_cols(heads[1], h), head_cols(heads[2], h), allowed)
        for h in range(local_heads)
    ]
    att_flat = jnp.concatenate([f[0] for f in fwd], axis=1)

    layer_out = chip_layer_out(att_flat, w_out).astype(jnp.bfloat16)[None]

    g_flat = lax.dot_general(
        grad_full, w_out, (((1,), (1,)), ((), ())), preferred_element_type=jnp.float32
    ).astype(jnp.bfloat16)
    att_blocks = att_flat.reshape(n_seq, nodes_here, local_heads * HD)
    grad_blocks = grad_full.reshape(n_seq, nodes_here, width)
    terms = jnp.einsum(
        "bnf,bnk->bfk", att_blocks, grad_blocks, preferred_element_type=jnp.float32
    ).astype(jnp.bfloat16)
    w_rows = jnp.sum(terms.astype(jnp.float32), axis=0)
    w_rows = lax.psum(w_rows.astype(jnp.bfloat16), "dp").astype(jnp.float32)
    batch = asking_vectors_matrix.shape[0] * lax.axis_size("dp")
    w_out_grad = w_rows / batch

    bwd = [
        attend_back(
            head_cols(heads[0], h),
            head_cols(heads[1], h),
            head_cols(heads[2], h),
            head_cols(g_flat, h),
            fwd[h][0],
            fwd[h][1],
            fwd[h][2],
        )
        for h in range(local_heads)
    ]
    grads = jnp.stack(
        [jnp.concatenate([b[i] for b in bwd], axis=1).reshape(groups, nodes_here, group_width)
         for i in range(3)]
    )
    back = lax.all_to_all(grads, "seq", split_axis=1, concat_axis=1, tiled=True)
    back = back.transpose(0, 2, 1, 3).reshape(3, 1, nodes_here, width)
    return (layer_out, back[0], back[1], back[2], w_out_grad)


def solution(mesh):
    return jax.shard_map(
        shards,
        mesh=mesh,
        in_specs=(
            P("dp", "seq", None),
            P("dp", "seq", None),
            P("dp", "seq", None),
            P("dp", "seq", None),
            P("seq", None),
            P("dp", None),
            P("dp", None),
        ),
        out_specs=(
            P("dp", "seq", None),
            P("dp", "seq", None),
            P("dp", "seq", None),
            P("dp", "seq", None),
            P("seq", None),
        ),
        check_vma=False,
    )
```
